256 devices in a mesh: seq: 64 (over z, y, x_lo), head: 4 (over x_hi, core).
Axes of the slice: x: 4 (x_hi: 2, x_lo: 2; x = x_hi * 2 + x_lo), y: 4, z: 8, core: 2. Of those that a mesh axis runs over, the one named last changes fastest.
Arguments:
- features: bfloat16 [8192, 960], P('seq', 'head'), may hold values from -36 to 36
- conv_weight: bfloat16 [960, 120, 128], P('head'), may hold values from -0.046875 to 0.046875
- ln_gain: float32 [960], replicated, may hold values from 0.5 to 1.5
- ln_bias: float32 [960], replicated, may hold values from -4 to 4
- query_weight: bfloat16 [8, 115200], P('head'), may hold values from -0.875 to 0.875
- key_weight: bfloat16 [8, 115200], P('head'), may hold values from -0.875 to 0.875
- value_weight: bfloat16 [8, 115200], P('head'), may hold values from -0.1875 to 0.1875
- out_weight: bfloat16 [960, 960], P('head'), may hold values from -0.1875 to 0.1875
- proj_weight: bfloat16 [960, 1024], P(None, 'head'), may hold values from -0.10085894 to 0.10085894
- targets: bfloat16 [8192, 1024], P('seq', 'head'), may hold values from -3.125 to 3.125
- mask_positions: int32 [1024], P('seq'), may hold values from 0 to 8191, as said below
- distractors: int32 [1024, 100], P('seq'), may hold values from 0 to 8191, as said below
- loss_weight: float32 [1024], P('seq'), may hold values from 0.2 to 2
Outputs:
- encoded: bfloat16 [8192, 960], P('seq', 'head')
- proj_grad: float32 [960, 1024], P(None, 'head')
- target_grad: float32 [8192, 1024], P('seq', 'head')
The draws below stay inside these ranges and needn't reach their ends.
Inputs may be any that keep to these rules, and one draw needn't show every extreme that they name: `mask_positions`: the entries of aligned block d of 16 are distinct frames of d * 128 to (d + 1) * 128 - 1. `distractors`: call value // 128 the block of an entry. In every aligned block of 16 rows exactly 50 entries name one block, the same block for all row blocks and drawn from the seed; the remaining 16 * 100 - 50 entries of the row block are spread over the other blocks as evenly as possible.
All inputs are finite; a program needn't handle non-finite values.
Results may differ from the reference program's by a relative error of at most 0.007.
Values may be sent and summed in bfloat16 or wider, within the bound.
No kernel may reach another device: no remote copies, remote signals or barrier semaphores. Data moves between devices by JAX's collectives and lax.ppermute only.
A program may use at most 128 MiB of HBM per device.

```python
import math
import jax
import jax.numpy as jnp
from jax import lax

HEADS = 8
HEAD_DIM = 120
FINAL = 1024
TAPS = 128
DISTRACT = 100
FRAMES = 128
WIDTH = 960
MASKED = 16
TOTAL = 8192
N_SEQ = 64


def scale_factors(key, count, lowest, highest):
    return jnp.exp(jax.random.uniform(key, (count,), jnp.float32, math.log(lowest), math.log(highest)))


def rough_matrix(key, row_count, col_count, lowest, highest):
    key_base, key_rows, key_cols = jax.random.split(key, 3)
    raw_values = jax.random.normal(key_base, (row_count, col_count), jnp.float32)
    raw_values = jnp.clip(raw_values, -4.0, 4.0)
    return raw_values * scale_factors(key_rows, row_count, lowest, highest)[:, None] * scale_factors(key_cols, col_count, lowest, highest)[None, :]


def draw_features(key, part):
    return rough_matrix(key, TOTAL, WIDTH, 0.3, 3.0).astype(jnp.bfloat16)


def draw_targets(key, part):
    return (rough_matrix(key, TOTAL, FINAL, 1.0, 10.0) / (4.0 * math.sqrt(FINAL))).astype(jnp.bfloat16)


def draw_proj_weight(key, part):
    return (rough_matrix(key, WIDTH, FINAL, 1.0, 10.0) / (4.0 * math.sqrt(WIDTH * FINAL))).astype(jnp.bfloat16)


def draw_mask_positions(key, part):
    block_total = TOTAL // FRAMES

    def per_block(block_index):
        chosen = jax.random.permutation(jax.random.fold_in(key, block_index), FRAMES)[:MASKED]
        return chosen.astype(jnp.int32) + block_index * FRAMES
    return jax.vmap(per_block)(jnp.arange(block_total, dtype=jnp.int32)).reshape(-1).astype(jnp.int32)


def draw_distractors(key, part):
    block_total = TOTAL // FRAMES
    request_count = MASKED * DISTRACT
    capacity = 2 * request_count // block_total
    remaining = request_count - capacity
    base_load = remaining // (block_total - 1)
    extra_load = remaining % (block_total - 1)
    busiest = jax.random.randint(jax.random.fold_in(key, 7), (), 0, block_total).astype(jnp.int32)
    owner_list = jnp.arange(block_total, dtype=jnp.int32)

    def per_block(block_index):
        sub_key = jax.random.fold_in(jax.random.fold_in(key, 1000), block_index)
        key_order, key_shuffle, key_rows = jax.random.split(sub_key, 3)
        shuffled = jax.random.permutation(key_order, block_total).astype(jnp.int32)
        position = jnp.argsort(shuffled, stable=True).astype(jnp.int32)
        ranking = position - (position > position[busiest]).astype(jnp.int32)
        block_loads = jnp.where(owner_list == busiest, capacity, base_load + (ranking < extra_load).astype(jnp.int32))
        load_ends = jnp.cumsum(block_loads)
        slot_ids = jnp.arange(request_count, dtype=jnp.int32)
        owners = jnp.sum((slot_ids[:, None] >= load_ends[None, :]).astype(jnp.int32), axis=1)
        owners = jax.random.permutation(key_shuffle, owners)
        row_ids = jax.random.randint(key_rows, (request_count,), 0, FRAMES).astype(jnp.int32)
        return (owners * FRAMES + row_ids).reshape(MASKED, DISTRACT)
    return jax.vmap(per_block)(jnp.arange(block_total, dtype=jnp.int32)).reshape(block_total * MASKED, DISTRACT).astype(jnp.int32)


def steps_of(own_key, extent, cuts, least, largest):
    factor_of = 1.0
    for dim, parts in cuts:
        steps = jax.random.uniform(jax.random.fold_in(jax.random.fold_in(own_key, 6), dim), (parts,), jnp.float32, least / len(cuts), largest / len(cuts))
        factor_of = factor_of * jnp.repeat(jnp.exp(steps), extent[dim] // parts).reshape((-1,) + (1,) * (len(extent) - 1 - dim))
    return factor_of


def bell_draw(rng, dims, width, reach, cuts=(), kind=jnp.bfloat16):
    entries = width * jax.random.normal(rng, dims, jnp.float32)
    if cuts:
        entries = entries * steps_of(rng, dims, cuts, -0.22, 0.18)
    return jnp.clip(entries, -reach, reach).astype(kind)


def setup_inputs(seed: int = 0) -> dict:
    seeds = jax.random.split(jax.random.key(seed), 14)
    return {
        "features": draw_features(jax.random.fold_in(seeds[13], 71), 0),
        "conv_weight": bell_draw(seeds[1], (WIDTH, HEAD_DIM, TAPS), (TAPS * HEAD_DIM) ** -0.5, 0.046875, ((0, 4),)),
        "ln_gain": jnp.clip(1.0 + 0.1 * jax.random.normal(seeds[2], (WIDTH,), jnp.float32), 0.5, 1.5),
        "ln_bias": bell_draw(seeds[3], (WIDTH,), 0.3, 4.0, (), jnp.float32),
        "query_weight": bell_draw(seeds[4], (HEADS, WIDTH * HEAD_DIM), (1.7 * WIDTH ** -0.5), 0.875, ((0, 4),)),
        "key_weight": bell_draw(seeds[5], (HEADS, WIDTH * HEAD_DIM), (1.7 * WIDTH ** -0.5), 0.875, ((0, 4),)),
        "value_weight": bell_draw(seeds[6], (HEADS, WIDTH * HEAD_DIM), WIDTH ** -0.5, 0.1875, ((0, 4),)),
        "out_weight": bell_draw(seeds[7], (WIDTH, WIDTH), WIDTH ** -0.5, 0.1875, ((0, 4),)),
        "proj_weight": draw_proj_weight(jax.random.fold_in(seeds[13], 71), 0),
        "targets": draw_targets(jax.random.fold_in(seeds[13], 71), 0),
        "mask_positions": draw_mask_positions(jax.random.fold_in(seeds[13], 71), 0),
        "distractors": draw_distractors(jax.random.fold_in(seeds[13], 71), 0),
        "loss_weight": jnp.clip(jnp.exp(math.log(2.0) - 2.3025851 * jax.random.uniform(seeds[12], (N_SEQ * MASKED,), jnp.float32) ** steps_of(seeds[12], (N_SEQ * MASKED,), ((0, 64),), -0.2, 0.2)), 0.2, 2.0),
    }


NORM_EPS = 1e-05
EPSILON = 1e-06
SOFTMAX_WARMTH = 0.1

def layer_norm(hidden, gain_terms, bias_terms):
    wide = hidden.astype(jnp.float32)
    center = lax.optimization_barrier(jnp.mean(wide, axis=-1, keepdims=True))
    spread = lax.optimization_barrier(jnp.mean((wide - center) ** 2, axis=-1, keepdims=True))
    return ((wide - center) * lax.rsqrt(spread + NORM_EPS) * gain_terms + bias_terms).astype(jnp.bfloat16)

def head_project(normed, flat_weight):
    head_weight = flat_weight.reshape(HEADS, WIDTH, HEAD_DIM).astype(jnp.float32)
    result = jnp.einsum('tw,hwd->thd', normed.astype(jnp.float32), head_weight, precision=lax.Precision.HIGHEST)
    return result.reshape(normed.shape[0], HEADS * HEAD_DIM).astype(jnp.bfloat16)

def contrast_grads(context, cands, products, target_sq, context_sq, weight_matrix):
    inv_context = lax.rsqrt(context_sq + EPSILON)
    inv_target = lax.rsqrt(target_sq + EPSILON)
    cosine_scores = products * inv_context[:, None] * inv_target
    exponentiated = jnp.exp(cosine_scores / SOFTMAX_WARMTH)
    softmax_shares = exponentiated / lax.optimization_barrier(jnp.sum(exponentiated, axis=1, keepdims=True))
    leading_term = (lax.broadcasted_iota(jnp.int32, softmax_shares.shape, 1) == 0).astype(jnp.float32)
    logit_slope = weight_matrix[:, None] * (softmax_shares - leading_term) / SOFTMAX_WARMTH
    along = logit_slope * inv_context[:, None] * inv_target
    shrink = logit_slope * cosine_scores * inv_target * inv_target
    spread = lax.optimization_barrier(jnp.sum(logit_slope * cosine_scores, axis=1)) * inv_context * inv_context
    cand_grads = along[:, :, None] * context[:, None, :] - shrink[:, :, None] * cands
    context_grad = jnp.einsum('mk,mke->me', along, cands, precision=lax.Precision.HIGHEST) - spread[:, None] * context
    return (cand_grads, context_grad)

def attention(queries, key_all, value_all):
    total_rows = queries.shape[0]
    block_rows = math.gcd(total_rows, 512)
    score_scale = 1.0 / math.sqrt(HEAD_DIM)
    key_heads = key_all.reshape(total_rows, HEADS, HEAD_DIM).astype(jnp.float32)
    value_heads = value_all.reshape(total_rows, HEADS, HEAD_DIM).astype(jnp.float32)
    query_blocks = queries.reshape(total_rows // block_rows, block_rows, HEADS, HEAD_DIM)

    def per_block(query_block):
        scores = jnp.einsum('qhd,khd->hqk', query_block.astype(jnp.float32), key_heads) * score_scale
        highest = lax.optimization_barrier(jnp.max(scores, axis=2, keepdims=True))
        weights = jnp.exp(scores - highest)
        totals = lax.optimization_barrier(jnp.sum(weights, axis=2))
        probs = lax.optimization_barrier(weights.astype(jnp.bfloat16)).astype(jnp.float32)
        numer = jnp.einsum('hqk,khd->hqd', probs, value_heads)
        return (numer / totals[:, :, None]).astype(jnp.bfloat16)
    outputs = lax.map(per_block, query_blocks)
    return outputs.transpose(0, 2, 1, 3).reshape(total_rows, HEADS * HEAD_DIM)

def reference(features, conv_weight, ln_gain, ln_bias, query_weight, key_weight, value_weight, out_weight, proj_weight, targets, mask_positions, distractors, loss_weight):
    half_taps = TAPS // 2
    position = lax.conv_general_dilated(features[None], conv_weight, (1,), [(half_taps, half_taps - 1)], dimension_numbers=('NWC', 'OIW', 'NWC'), feature_group_count=HEADS, preferred_element_type=jnp.float32)[0]
    hidden = (features.astype(jnp.float32) + jax.nn.gelu(position, approximate=False)).astype(jnp.bfloat16)
    normed = layer_norm(hidden, ln_gain, ln_bias)
    queries = head_project(normed, query_weight)
    key_all = head_project(normed, key_weight)
    value_all = head_project(normed, value_weight)
    attended = attention(queries, key_all, value_all)
    encoded = (hidden.astype(jnp.float32) + jnp.dot(attended, out_weight, preferred_element_type=jnp.float32)).astype(jnp.bfloat16)
    mask_blocks = mask_positions.reshape(N_SEQ, MASKED)
    dist_blocks = distractors.reshape(N_SEQ, MASKED, DISTRACT)
    weight_blocks = loss_weight.reshape(N_SEQ, MASKED)

    def per_device(running, inputs):
        target_grad, proj_grad = running
        block_mask, block_dist, block_weight = inputs
        chosen = encoded[block_mask]
        context = jnp.dot(chosen, proj_weight, preferred_element_type=jnp.float32)
        indices = jnp.concatenate([block_mask[:, None], block_dist], axis=1).astype(jnp.int32)
        cands = targets[indices].astype(jnp.float32)
        products = jnp.einsum('me,mke->mk', context, cands, precision=lax.Precision.HIGHEST)
        target_sq = lax.optimization_barrier(jnp.sum(cands * cands, axis=2))
        context_sq = lax.optimization_barrier(jnp.sum(context * context, axis=1))
        cand_grads, context_grad = contrast_grads(context, cands, products, target_sq, context_sq, block_weight)
        proj_grad = proj_grad + jnp.einsum('mw,me->we', chosen.astype(jnp.float32), context_grad, precision=lax.Precision.HIGHEST)
        target_grad = target_grad.at[indices.reshape(-1)].add(cand_grads.reshape(-1, FINAL))
        return ((target_grad, proj_grad), None)
    initial = (jnp.zeros((TOTAL, FINAL), jnp.float32), jnp.zeros((WIDTH, FINAL), jnp.float32))
    (target_grad, proj_grad), _ = lax.scan(per_device, initial, (mask_blocks, dist_blocks, weight_blocks))
    return (encoded, proj_grad, target_grad)
```

```python
import math

import jax
import jax.numpy as jnp
from jax import lax
from jax.sharding import PartitionSpec as P

TAPS = 128


NORM_EPS = 1e-05
EPSILON = 1e-06
SOFTMAX_WARMTH = 0.1


def with_halo(shard, sides, width):
    for axis, dim in sides:
        size, length = (lax.axis_size(axis), shard.shape[dim])
        up = [(i, (i + 1) % size) for i in range(size - 1)]
        down = [(j, i) for i, j in up]
        last = lax.slice_in_dim(shard, length - width, length, axis=dim)
        first = lax.slice_in_dim(shard, 0, width, axis=dim)
        before = lax.ppermute(last, axis, up)
        after = lax.ppermute(first, axis, down)
        shard = jnp.concatenate([before, shard, after], axis=dim)
    return shard


def layer_norm(hidden, gain_terms, bias_terms):
    wide = hidden.astype(jnp.float32)
    center = jnp.mean(wide, axis=-1, keepdims=True)
    spread = jnp.mean((wide - center) ** 2, axis=-1, keepdims=True)
    return ((wide - center) * lax.rsqrt(spread + NORM_EPS) * gain_terms + bias_terms).astype(
        jnp.bfloat16
    )


def head_project(normed, flat_weight, head_count, head_dim):
    full_width = normed.shape[1]
    head_weight = flat_weight.reshape(head_count, full_width, head_dim)
    result = jnp.einsum("tw,hwd->thd", normed, head_weight, preferred_element_type=jnp.float32)
    return result.astype(jnp.bfloat16)


def contrast_terms(products, target_sq, context_sq, weight_matrix):
    inv_context = lax.rsqrt(context_sq + EPSILON)
    inv_target = lax.rsqrt(target_sq + EPSILON)
    cosine_scores = products * inv_context[:, None] * inv_target
    exponentiated = jnp.exp(cosine_scores / SOFTMAX_WARMTH)
    softmax_shares = exponentiated / jnp.sum(exponentiated, axis=1, keepdims=True)
    leading_term = (lax.broadcasted_iota(jnp.int32, softmax_shares.shape, 1) == 0).astype(
        jnp.float32
    )
    logit_slope = weight_matrix[:, None] * (softmax_shares - leading_term) / SOFTMAX_WARMTH
    along = logit_slope * inv_context[:, None] * inv_target
    shrink = logit_slope * cosine_scores * inv_target * inv_target
    spread = jnp.sum(logit_slope * cosine_scores, axis=1) * inv_context * inv_context
    return (along, shrink, spread)


def attend_block(running, key_block, value_block, query_heads, head_count, score_scale):
    numer, denom, highest = running
    row_count = key_block.shape[0]
    key_heads = key_block.reshape(row_count, head_count, -1)
    value_heads = value_block.reshape(row_count, head_count, -1)
    scores = (
        jnp.einsum("qhd,khd->hqk", query_heads, key_heads, preferred_element_type=jnp.float32)
        * score_scale
    )
    new_high = jnp.maximum(highest, jnp.max(scores, axis=2))
    factor = jnp.exp(highest - new_high)
    weights = jnp.exp(scores - new_high[:, :, None])
    denom = denom * factor + jnp.sum(weights, axis=2)
    numer = numer * factor[:, :, None] + jnp.einsum(
        "hqk,khd->hqd",
        weights.astype(jnp.bfloat16),
        value_heads,
        preferred_element_type=jnp.float32,
    )
    return (numer, denom, new_high)


def take_rows(asked, targets):
    return targets[jnp.maximum(asked, 0)]


def place_rows(asked_flat, rows_flat, frame_count):
    segment_ids = jnp.where(asked_flat >= 0, asked_flat, frame_count)
    return jax.ops.segment_sum(rows_flat, segment_ids, num_segments=frame_count + 1)[:frame_count]


def seq_sum(term, axis):
    size = lax.axis_size(axis)
    rows, cols = term.shape
    chunk = -(-rows // size)
    padded = jnp.pad(term, ((0, chunk * size - rows), (0, 0))).reshape(size, chunk, cols)
    reduced = lax.all_to_all(padded, axis, 0, 0, tiled=True).sum(axis=0)
    copies = jnp.broadcast_to(reduced[None], (size, chunk, cols))
    gathered = lax.all_to_all(copies, axis, 0, 0, tiled=True)
    return gathered.reshape(size * chunk, cols)[:rows]


def per_device(
    features,
    conv_weight,
    ln_gain,
    ln_bias,
    query_weight,
    key_weight,
    value_weight,
    out_weight,
    proj_weight,
    targets,
    mask_positions,
    distractors,
    loss_weight,
):
    frame_count, local_width = features.shape
    head_dim = conv_weight.shape[1]
    head_count = local_width // head_dim
    extended = with_halo(features, (("seq", 0),), TAPS // 2)
    position = lax.conv_general_dilated(
        extended[None],
        conv_weight,
        (1,),
        "VALID",
        dimension_numbers=("NWC", "OIW", "NWC"),
        feature_group_count=head_count,
        preferred_element_type=jnp.float32,
    )[0, :frame_count]
    hidden = (features.astype(jnp.float32) + jax.nn.gelu(position, approximate=False)).astype(
        jnp.bfloat16
    )
    normed = layer_norm(lax.all_gather(hidden, "head", axis=1, tiled=True), ln_gain, ln_bias)
    query_heads = head_project(normed, query_weight, head_count, head_dim)
    key_here = head_project(normed, key_weight, head_count, head_dim).reshape(
        frame_count, local_width
    )
    value_here = head_project(normed, value_weight, head_count, head_dim).reshape(
        frame_count, local_width
    )
    score_scale = 1.0 / math.sqrt(head_dim)
    initial = (
        jnp.zeros((head_count, frame_count, head_dim), jnp.float32),
        jnp.zeros((head_count, frame_count), jnp.float32),
        jnp.full((head_count, frame_count), -1e30, jnp.float32),
    )
    running = initial
    seq_total = lax.axis_size("seq")
    kv_here = jnp.concatenate([key_here, value_here], axis=1)
    kv_copies = jnp.broadcast_to(kv_here[None], (seq_total,) + kv_here.shape).reshape(
        seq_total * frame_count, 2 * local_width
    )
    kv_all = lax.all_to_all(kv_copies, "seq", 0, 0, tiled=True)
    key_piece = kv_all[:, :local_width]
    value_piece = kv_all[:, local_width:]
    row_count = key_piece.shape[0]

    def advance(partial_value, blocks):
        return (
            attend_block(partial_value, blocks[0], blocks[1], query_heads, head_count, score_scale),
            None,
        )

    running, _ = lax.scan(
        advance,
        running,
        (
            key_piece.reshape(row_count // 512, 512, -1),
            value_piece.reshape(row_count // 512, 512, -1),
        ),
    )
    numer, denom, _ = running
    attended = (
        (numer / denom[:, :, None])
        .astype(jnp.bfloat16)
        .transpose(1, 0, 2)
        .reshape(frame_count, local_width)
    )
    branch = lax.psum_scatter(
        jnp.dot(attended, out_weight, preferred_element_type=jnp.float32).astype(jnp.bfloat16),
        "head",
        scatter_dimension=1,
        tiled=True,
    ).astype(jnp.float32)
    encoded = (hidden.astype(jnp.float32) + branch).astype(jnp.bfloat16)
    seq_index = lax.axis_index("seq")
    seq_count = lax.axis_size("seq")
    local_mask = mask_positions - seq_index * frame_count
    masked_full = lax.all_gather(encoded[local_mask], "head", axis=1, tiled=True)
    context = jnp.dot(masked_full, proj_weight, preferred_element_type=jnp.float32)
    masked_count, distract_count = distractors.shape
    request_count = masked_count * distract_count
    capacity = 2 * request_count // seq_count
    target_width = targets.shape[1]
    flat_dist = distractors.reshape(-1)
    owners = flat_dist // frame_count
    row_ids = flat_dist % frame_count
    owner_hits = (owners[:, None] == jnp.arange(seq_count, dtype=jnp.int32)[None, :]).astype(
        jnp.int32
    )
    earlier = jnp.cumsum(owner_hits, axis=0) - owner_hits
    slot_ids = jnp.sum(earlier * owner_hits, axis=1)
    buckets = owners * capacity + slot_ids
    requests = (
        jnp.full((seq_count * capacity,), -1, jnp.int32)
        .at[buckets]
        .set(row_ids)
        .reshape(seq_count, capacity)
    )
    positive = targets[local_mask]
    asked = lax.all_to_all(requests, "seq", split_axis=0, concat_axis=0, tiled=True)
    found = take_rows(asked, targets)
    returned = lax.all_to_all(found, "seq", split_axis=0, concat_axis=0, tiled=True)
    fetched = returned.reshape(seq_count * capacity, target_width)[buckets].reshape(
        masked_count, distract_count, target_width
    )
    cands = jnp.concatenate([positive[:, None, :], fetched], axis=1).astype(jnp.float32)
    products_here = jnp.einsum("me,mke->mk", context, cands, precision=lax.Precision.HIGHEST)
    target_sq_here = jnp.sum(cands * cands, axis=2)
    context_sq_here = jnp.sum(context * context, axis=1)
    products, target_sq, context_sq = lax.psum(
        (products_here, target_sq_here, context_sq_here), "head"
    )
    along, shrink, spread = contrast_terms(products, target_sq, context_sq, loss_weight)
    cand_grads = along[:, :, None] * context[:, None, :] - shrink[:, :, None] * cands
    context_grad = (
        jnp.einsum("mk,mke->me", along, cands, precision=lax.Precision.HIGHEST)
        - spread[:, None] * context
    )
    target_grad = (
        jnp.zeros((frame_count, target_width), jnp.float32).at[local_mask].add(cand_grads[:, 0])
    )
    outgoing = (
        jnp.zeros((seq_count * capacity, target_width), jnp.float32)
        .at[buckets]
        .set(cand_grads[:, 1:].reshape(request_count, target_width))
    )
    incoming = (
        lax.all_to_all(
            outgoing.reshape(seq_count, capacity, target_width).astype(jnp.bfloat16),
            "seq",
            split_axis=0,
            concat_axis=0,
            tiled=True,
        )
        .astype(jnp.float32)
        .reshape(seq_count * capacity, target_width)
    )
    target_grad = target_grad + place_rows(asked.reshape(-1), incoming, frame_count)
    proj_term = jnp.einsum(
        "mw,me->we", masked_full.astype(jnp.float32), context_grad, precision=lax.Precision.HIGHEST
    )
    proj_grad = seq_sum(proj_term, "seq")
    return (encoded, proj_grad, target_grad)


def solution(mesh):
    return jax.shard_map(
        per_device,
        mesh=mesh,
        in_specs=(
            P("seq", "head"),
            P("head", None, None),
            P(),
            P(),
            P("head", None),
            P("head", None),
            P("head", None),
            P("head", None),
            P(None, "head"),
            P("seq", "head"),
            P("seq"),
            P("seq", None),
            P("seq"),
        ),
        out_specs=(P("seq", "head"), P(None, "head"), P("seq", "head")),
        check_vma=False,
    )
```

```python
import math

import jax
import jax.numpy as jnp
from jax import lax
from jax.sharding import Mesh, PartitionSpec as P

TAPS = 128
SEQ = ("sz", "sx")


NORM_EPS = 1e-05
EPSILON = 1e-06
SOFTMAX_WARMTH = 0.1


def with_halo(shard, sides, width):
    for axis, dim in sides:
        size, length = (lax.axis_size(axis), shard.shape[dim])
        up = [(i, (i + 1) % size) for i in range(size - 1)]
        down = [(j, i) for i, j in up]
        last = lax.slice_in_dim(shard, length - width, length, axis=dim)
        first = lax.slice_in_dim(shard, 0, width, axis=dim)
        before = lax.ppermute(last, axis, up)
        after = lax.ppermute(first, axis, down)
        shard = jnp.concatenate([before, shard, after], axis=dim)
    return shard


def layer_norm(hidden, gain_terms, bias_terms):
    wide = hidden.astype(jnp.float32)
    center = jnp.mean(wide, axis=-1, keepdims=True)
    spread = jnp.mean((wide - center) ** 2, axis=-1, keepdims=True)
    return ((wide - center) * lax.rsqrt(spread + NORM_EPS) * gain_terms + bias_terms).astype(
        jnp.bfloat16
    )


def head_project(normed, flat_weight, head_count, head_dim):
    full_width = normed.shape[1]
    head_weight = flat_weight.reshape(head_count, full_width, head_dim)
    result = jnp.einsum("tw,hwd->thd", normed, head_weight, preferred_element_type=jnp.float32)
    return result.astype(jnp.bfloat16)


def contrast_terms(products, target_sq, context_sq, weight_matrix):
    inv_context = lax.rsqrt(context_sq + EPSILON)
    inv_target = lax.rsqrt(target_sq + EPSILON)
    cosine_scores = products * inv_context[:, None] * inv_target
    exponentiated = jnp.exp(cosine_scores / SOFTMAX_WARMTH)
    softmax_shares = exponentiated / jnp.sum(exponentiated, axis=1, keepdims=True)
    leading_term = (lax.broadcasted_iota(jnp.int32, softmax_shares.shape, 1) == 0).astype(
        jnp.float32
    )
    logit_slope = weight_matrix[:, None] * (softmax_shares - leading_term) / SOFTMAX_WARMTH
    along = logit_slope * inv_context[:, None] * inv_target
    shrink = logit_slope * cosine_scores * inv_target * inv_target
    spread = jnp.sum(logit_slope * cosine_scores, axis=1) * inv_context * inv_context
    return (along, shrink, spread)


def attend_block(running, key_block, value_block, query_heads, head_count, score_scale):
    numer, denom, highest = running
    row_count = key_block.shape[0]
    key_heads = key_block.reshape(row_count, head_count, -1)
    value_heads = value_block.reshape(row_count, head_count, -1)
    scores = (
        jnp.einsum("qhd,khd->hqk", query_heads, key_heads, preferred_element_type=jnp.float32)
        * score_scale
    )
    new_high = jnp.maximum(highest, jnp.max(scores, axis=2))
    factor = jnp.exp(highest - new_high)
    weights = jnp.exp(scores - new_high[:, :, None])
    denom = denom * factor + jnp.sum(weights, axis=2)
    numer = numer * factor[:, :, None] + jnp.einsum(
        "hqk,khd->hqd",
        weights.astype(jnp.bfloat16),
        value_heads,
        preferred_element_type=jnp.float32,
    )
    return (numer, denom, new_high)


def take_rows(asked, targets):
    return targets[jnp.maximum(asked, 0)]


def place_rows(asked_flat, rows_flat, frame_count):
    segment_ids = jnp.where(asked_flat >= 0, asked_flat, frame_count)
    return jax.ops.segment_sum(rows_flat, segment_ids, num_segments=frame_count + 1)[:frame_count]


def seq_sum(term, axis):
    size = lax.axis_size(axis)
    rows, cols = term.shape
    chunk = -(-rows // size)
    padded = jnp.pad(term, ((0, chunk * size - rows), (0, 0))).reshape(size, chunk, cols)
    reduced = lax.all_to_all(padded, axis, 0, 0, tiled=True).sum(axis=0)
    copies = jnp.broadcast_to(reduced[None], (size, chunk, cols))
    gathered = lax.all_to_all(copies, axis, 0, 0, tiled=True)
    return gathered.reshape(size * chunk, cols)[:rows]


def per_device(
    features,
    conv_weight,
    ln_gain,
    ln_bias,
    query_weight,
    key_weight,
    value_weight,
    out_weight,
    proj_weight,
    targets,
    mask_positions,
    distractors,
    loss_weight,
):
    frame_count, local_width = features.shape
    head_dim = conv_weight.shape[1]
    head_count = local_width // head_dim
    extended = with_halo(features, ((SEQ, 0),), TAPS // 2)
    position = lax.conv_general_dilated(
        extended[None],
        conv_weight,
        (1,),
        "VALID",
        dimension_numbers=("NWC", "OIW", "NWC"),
        feature_group_count=head_count,
        preferred_element_type=jnp.float32,
    )[0, :frame_count]
    hidden = (features.astype(jnp.float32) + jax.nn.gelu(position, approximate=False)).astype(
        jnp.bfloat16
    )
    normed = layer_norm(lax.all_gather(hidden, "head", axis=1, tiled=True), ln_gain, ln_bias)
    query_here = head_project(normed, query_weight, head_count, head_dim).reshape(
        frame_count, local_width
    )
    key_here = head_project(normed, key_weight, head_count, head_dim).reshape(
        frame_count, local_width
    )
    value_here = head_project(normed, value_weight, head_count, head_dim).reshape(
        frame_count, local_width
    )
    side = lax.axis_index("sx")
    swap = [(0, 1), (1, 0)]
    qkv = jnp.stack([query_here, key_here, value_here]).reshape(3, frame_count, head_count, head_dim)
    mine = jnp.where(side == 0, qkv[:, :, 0], qkv[:, :, 1])
    theirs = jnp.where(side == 0, qkv[:, :, 1], qkv[:, :, 0])
    received = lax.ppermute(theirs, "sx", swap)
    pair = jnp.concatenate([mine, received], axis=1)
    kv_pair = jnp.concatenate([pair[1], pair[2]], axis=1)
    kv_all = lax.all_gather(kv_pair, "sz", axis=0, tiled=True)
    key_piece = kv_all[:, :head_dim]
    value_piece = kv_all[:, head_dim:]
    query_heads = pair[0][:, None, :]
    pair_rows = 2 * frame_count
    score_scale = 1.0 / math.sqrt(head_dim)
    running = (
        jnp.zeros((1, pair_rows, head_dim), jnp.float32),
        jnp.zeros((1, pair_rows), jnp.float32),
        jnp.full((1, pair_rows), -1e30, jnp.float32),
    )
    row_count = key_piece.shape[0]

    def advance(partial_value, blocks):
        return (
            attend_block(partial_value, blocks[0], blocks[1], query_heads, 1, score_scale),
            None,
        )

    running, _ = lax.scan(
        advance,
        running,
        (
            key_piece.reshape(row_count // 512, 512, -1),
            value_piece.reshape(row_count // 512, 512, -1),
        ),
    )
    numer, denom, _ = running
    attended_pair = (numer / denom[:, :, None]).astype(jnp.bfloat16)[0]
    own_part = attended_pair[:frame_count]
    back = lax.ppermute(attended_pair[frame_count:], "sx", swap)
    attended = jnp.where(
        side == 0,
        jnp.concatenate([own_part, back], axis=1),
        jnp.concatenate([back, own_part], axis=1),
    )
    branch = lax.psum_scatter(
        jnp.dot(attended, out_weight, preferred_element_type=jnp.float32).astype(jnp.bfloat16),
        "head",
        scatter_dimension=1,
        tiled=True,
    ).astype(jnp.float32)
    encoded = (hidden.astype(jnp.float32) + branch).astype(jnp.bfloat16)
    seq_index = lax.axis_index(SEQ)
    seq_count = lax.axis_size(SEQ)
    local_mask = mask_positions - seq_index * frame_count
    masked_full = lax.all_gather(encoded[local_mask], "head", axis=1, tiled=True)
    context = jnp.dot(masked_full, proj_weight, preferred_element_type=jnp.float32)
    masked_count, distract_count = distractors.shape
    request_count = masked_count * distract_count
    capacity = 2 * request_count // seq_count
    target_width = targets.shape[1]
    flat_dist = distractors.reshape(-1)
    owners = flat_dist // frame_count
    row_ids = flat_dist % frame_count
    owner_hits = (owners[:, None] == jnp.arange(seq_count, dtype=jnp.int32)[None, :]).astype(
        jnp.int32
    )
    earlier = jnp.cumsum(owner_hits, axis=0) - owner_hits
    slot_ids = jnp.sum(earlier * owner_hits, axis=1)
    buckets = owners * capacity + slot_ids
    requests = (
        jnp.full((seq_count * capacity,), -1, jnp.int32)
        .at[buckets]
        .set(row_ids)
        .reshape(seq_count, capacity)
    )
    positive = targets[local_mask]
    asked = lax.all_to_all(requests, SEQ, split_axis=0, concat_axis=0, tiled=True)
    found = take_rows(asked, targets)
    returned = lax.all_to_all(found, SEQ, split_axis=0, concat_axis=0, tiled=True)
    fetched = returned.reshape(seq_count * capacity, target_width)[buckets].reshape(
        masked_count, distract_count, target_width
    )
    cands = jnp.concatenate([positive[:, None, :], fetched], axis=1).astype(jnp.float32)
    products_here = jnp.einsum("me,mke->mk", context, cands, precision=lax.Precision.HIGHEST)
    target_sq_here = jnp.sum(cands * cands, axis=2)
    context_sq_here = jnp.sum(context * context, axis=1)
    products, target_sq, context_sq = lax.psum(
        (products_here, target_sq_here, context_sq_here), "head"
    )
    along, shrink, spread = contrast_terms(products, target_sq, context_sq, loss_weight)
    cand_grads = along[:, :, None] * context[:, None, :] - shrink[:, :, None] * cands
    context_grad = (
        jnp.einsum("mk,mke->me", along, cands, precision=lax.Precision.HIGHEST)
        - spread[:, None] * context
    )
    target_grad = (
        jnp.zeros((frame_count, target_width), jnp.float32).at[local_mask].add(cand_grads[:, 0])
    )
    outgoing = (
        jnp.zeros((seq_count * capacity, target_width), jnp.float32)
        .at[buckets]
        .set(cand_grads[:, 1:].reshape(request_count, target_width))
    )
    incoming = (
        lax.all_to_all(
            outgoing.reshape(seq_count, capacity, target_width).astype(jnp.bfloat16),
            SEQ,
            split_axis=0,
            concat_axis=0,
            tiled=True,
        )
        .astype(jnp.float32)
        .reshape(seq_count * capacity, target_width)
    )
    target_grad = target_grad + place_rows(asked.reshape(-1), incoming, frame_count)
    proj_term = jnp.einsum(
        "mw,me->we", masked_full.astype(jnp.float32), context_grad, precision=lax.Precision.HIGHEST
    )
    proj_grad = seq_sum(proj_term, SEQ)
    return (encoded, proj_grad, target_grad)


def solution(mesh):
    seq_size, head_size = mesh.shape["seq"], mesh.shape["head"]
    split_mesh = Mesh(mesh.devices.reshape(seq_size // 2, 2, head_size), ("sz", "sx", "head"))
    return jax.shard_map(
        per_device,
        mesh=split_mesh,
        in_specs=(
            P(SEQ, "head"),
            P("head", None, None),
            P(),
            P(),
            P("head", None),
            P("head", None),
            P("head", None),
            P("head", None),
            P(None, "head"),
            P(SEQ, "head"),
            P(SEQ),
            P(SEQ, None),
            P(SEQ),
        ),
        out_specs=(P(SEQ, "head"), P(None, "head"), P(SEQ, "head")),
        check_vma=False,
    )
```

```python
import math

import jax
import jax.numpy as jnp
from jax import lax
from jax.sharding import Mesh, PartitionSpec as P

TAPS = 128
SEQ = ("sz", "sx")


NORM_EPS = 1e-05
EPSILON = 1e-06
SOFTMAX_WARMTH = 0.1


def with_halo(shard, sides, width):
    for axis, dim in sides:
        size, length = (lax.axis_size(axis), shard.shape[dim])
        up = [(i, (i + 1) % size) for i in range(size - 1)]
        down = [(j, i) for i, j in up]
        last = lax.slice_in_dim(shard, length - width, length, axis=dim)
        first = lax.slice_in_dim(shard, 0, width, axis=dim)
        before = lax.ppermute(last, axis, up)
        after = lax.ppermute(first, axis, down)
        shard = jnp.concatenate([before, shard, after], axis=dim)
    return shard


def layer_norm(hidden, gain_terms, bias_terms):
    wide = hidden.astype(jnp.float32)
    center = jnp.mean(wide, axis=-1, keepdims=True)
    spread = jnp.mean((wide - center) ** 2, axis=-1, keepdims=True)
    return ((wide - center) * lax.rsqrt(spread + NORM_EPS) * gain_terms + bias_terms).astype(
        jnp.bfloat16
    )


def head_project(normed, flat_weight, head_count, head_dim):
    full_width = normed.shape[1]
    head_weight = flat_weight.reshape(head_count, full_width, head_dim)
    result = jnp.einsum("tw,hwd->thd", normed, head_weight, preferred_element_type=jnp.float32)
    return result.astype(jnp.bfloat16)


def contrast_terms(products, target_sq, context_sq, weight_matrix):
    inv_context = lax.rsqrt(context_sq + EPSILON)
    inv_target = lax.rsqrt(target_sq + EPSILON)
    cosine_scores = products * inv_context[:, None] * inv_target
    exponentiated = jnp.exp(cosine_scores / SOFTMAX_WARMTH)
    softmax_shares = exponentiated / jnp.sum(exponentiated, axis=1, keepdims=True)
    leading_term = (lax.broadcasted_iota(jnp.int32, softmax_shares.shape, 1) == 0).astype(
        jnp.float32
    )
    logit_slope = weight_matrix[:, None] * (softmax_shares - leading_term) / SOFTMAX_WARMTH
    along = logit_slope * inv_context[:, None] * inv_target
    shrink = logit_slope * cosine_scores * inv_target * inv_target
    spread = jnp.sum(logit_slope * cosine_scores, axis=1) * inv_context * inv_context
    return (along, shrink, spread)


def attend_block(running, key_block, value_block, query_heads, head_count, score_scale):
    numer, denom, highest = running
    row_count = key_block.shape[0]
    key_heads = key_block.reshape(row_count, head_count, -1)
    value_heads = value_block.reshape(row_count, head_count, -1)
    scores = (
        jnp.einsum("qhd,khd->hqk", query_heads, key_heads, preferred_element_type=jnp.float32)
        * score_scale
    )
    new_high = jnp.maximum(highest, jnp.max(scores, axis=2))
    factor = jnp.exp(highest - new_high)
    weights = jnp.exp(scores - new_high[:, :, None])
    denom = denom * factor + jnp.sum(weights, axis=2)
    numer = numer * factor[:, :, None] + jnp.einsum(
        "hqk,khd->hqd",
        weights.astype(jnp.bfloat16),
        value_heads,
        preferred_element_type=jnp.float32,
    )
    return (numer, denom, new_high)


def take_rows(asked, targets):
    return targets[jnp.maximum(asked, 0)]


def place_rows(asked_flat, rows_flat, frame_count):
    segment_ids = jnp.where(asked_flat >= 0, asked_flat, frame_count)
    return jax.ops.segment_sum(rows_flat, segment_ids, num_segments=frame_count + 1)[:frame_count]


def seq_sum(term, axis):
    size = lax.axis_size(axis)
    rows, cols = term.shape
    chunk = -(-rows // size)
    padded = jnp.pad(term, ((0, chunk * size - rows), (0, 0))).reshape(size, chunk, cols)
    reduced = lax.all_to_all(padded, axis, 0, 0, tiled=True).sum(axis=0)
    copies = jnp.broadcast_to(reduced[None], (size, chunk, cols))
    gathered = lax.all_to_all(copies, axis, 0, 0, tiled=True)
    return gathered.reshape(size * chunk, cols)[:rows]


def per_device(
    features,
    conv_weight,
    ln_gain,
    ln_bias,
    query_weight,
    key_weight,
    value_weight,
    out_weight,
    proj_weight,
    targets,
    mask_positions,
    distractors,
    loss_weight,
):
    frame_count, local_width = features.shape
    head_dim = conv_weight.shape[1]
    head_count = local_width // head_dim
    extended = with_halo(features, ((SEQ, 0),), TAPS // 2)
    position = lax.conv_general_dilated(
        extended[None],
        conv_weight,
        (1,),
        "VALID",
        dimension_numbers=("NWC", "OIW", "NWC"),
        feature_group_count=head_count,
        preferred_element_type=jnp.float32,
    )[0, :frame_count]
    hidden = (features.astype(jnp.float32) + jax.nn.gelu(position, approximate=False)).astype(
        jnp.bfloat16
    )
    normed = layer_norm(lax.all_gather(hidden, "head", axis=1, tiled=True), ln_gain, ln_bias)
    query_here = head_project(normed, query_weight, head_count, head_dim).reshape(
        frame_count, local_width
    )
    key_here = head_project(normed, key_weight, head_count, head_dim).reshape(
        frame_count, local_width
    )
    value_here = head_project(normed, value_weight, head_count, head_dim).reshape(
        frame_count, local_width
    )
    side = lax.axis_index("sx")
    swap = [(0, 1), (1, 0)]
    qkv = jnp.stack([query_here, key_here, value_here]).reshape(3, frame_count, head_count, head_dim)
    mine = jnp.where(side == 0, qkv[:, :, 0], qkv[:, :, 1])
    theirs = jnp.where(side == 0, qkv[:, :, 1], qkv[:, :, 0])
    received = lax.ppermute(theirs, "sx", swap)
    pair = jnp.concatenate([mine, received], axis=1)
    kv_pair = jnp.concatenate([pair[1], pair[2]], axis=1)
    kv_all = lax.all_gather(kv_pair, "sz", axis=0, tiled=True)
    key_piece = kv_all[:, :head_dim]
    value_piece = kv_all[:, head_dim:]
    score_scale = 1.0 / math.sqrt(head_dim)
    scores = (
        jnp.einsum("qd,kd->qk", pair[0], key_piece, preferred_element_type=jnp.float32)
        * score_scale
    )
    highest = jnp.max(scores, axis=1, keepdims=True)
    weights = jnp.exp(scores - highest)
    totals = jnp.sum(weights, axis=1, keepdims=True)
    numer = jnp.dot(weights.astype(jnp.bfloat16), value_piece, preferred_element_type=jnp.float32)
    attended_pair = (numer / totals).astype(jnp.bfloat16)
    own_part = attended_pair[:frame_count]
    back = lax.ppermute(attended_pair[frame_count:], "sx", swap)
    attended = jnp.where(
        side == 0,
        jnp.concatenate([own_part, back], axis=1),
        jnp.concatenate([back, own_part], axis=1),
    )
    branch = lax.psum_scatter(
        jnp.dot(attended, out_weight, preferred_element_type=jnp.float32).astype(jnp.bfloat16),
        "head",
        scatter_dimension=1,
        tiled=True,
    ).astype(jnp.float32)
    encoded = (hidden.astype(jnp.float32) + branch).astype(jnp.bfloat16)
    seq_index = lax.axis_index(SEQ)
    seq_count = lax.axis_size(SEQ)
    local_mask = mask_positions - seq_index * frame_count
    masked_full = lax.all_gather(encoded[local_mask], "head", axis=1, tiled=True)
    context = jnp.dot(masked_full, proj_weight, preferred_element_type=jnp.float32)
    masked_count, distract_count = distractors.shape
    request_count = masked_count * distract_count
    capacity = 2 * request_count // seq_count
    target_width = targets.shape[1]
    flat_dist = distractors.reshape(-1)
    owners = flat_dist // frame_count
    row_ids = flat_dist % frame_count
    owner_hits = owners[:, None] == jnp.arange(seq_count, dtype=jnp.int32)[None, :]
    hits = owner_hits.astype(jnp.bfloat16).reshape(masked_count, distract_count, seq_count)
    before = lax.broadcasted_iota(jnp.int32, (distract_count,) * 2, 0) > lax.broadcasted_iota(
        jnp.int32, (distract_count,) * 2, 1
    )
    within = jnp.einsum(
        "kj,mjs->mks", before.astype(jnp.bfloat16), hits, preferred_element_type=jnp.float32
    )
    row_totals = jnp.sum(hits.astype(jnp.float32), axis=1)
    rows_before = lax.broadcasted_iota(jnp.int32, (masked_count,) * 2, 0) > lax.broadcasted_iota(
        jnp.int32, (masked_count,) * 2, 1
    )
    prior = jnp.dot(
        rows_before.astype(jnp.float32), row_totals, precision=lax.Precision.HIGHEST
    )
    earlier = (within + prior[:, None, :]).reshape(request_count, seq_count)
    slot_ids = jnp.sum(jnp.where(owner_hits, earlier, 0.0), axis=1).astype(jnp.int32)
    buckets = owners * capacity + slot_ids
    slot_total = seq_count * capacity
    place = lax.broadcasted_iota(jnp.int32, (slot_total, request_count), 0) == buckets[None, :]
    place_b = place.astype(jnp.bfloat16)
    requests = (
        jnp.sum(jnp.where(place, row_ids[None, :] + 1, 0), axis=1) - 1
    ).reshape(seq_count, capacity)
    positive = targets[local_mask]
    asked = lax.all_to_all(requests, SEQ, split_axis=0, concat_axis=0, tiled=True)
    pick = (
        asked.reshape(-1)[:, None] == jnp.arange(frame_count, dtype=jnp.int32)[None, :]
    ).astype(jnp.bfloat16)
    found = jnp.dot(pick, targets, preferred_element_type=jnp.float32).astype(jnp.bfloat16)
    returned = lax.all_to_all(
        found.reshape(seq_count, capacity, target_width),
        SEQ,
        split_axis=0,
        concat_axis=0,
        tiled=True,
    )
    fetched = jnp.einsum(
        "br,bw->rw",
        place_b,
        returned.reshape(slot_total, target_width),
        preferred_element_type=jnp.float32,
    ).reshape(masked_count, distract_count, target_width)
    cands = jnp.concatenate([positive[:, None, :], fetched], axis=1).astype(jnp.float32)
    products_here = jnp.einsum("me,mke->mk", context, cands, precision=lax.Precision.HIGHEST)
    target_sq_here = jnp.sum(cands * cands, axis=2)
    context_sq_here = jnp.sum(context * context, axis=1)
    products, target_sq, context_sq = lax.psum(
        (products_here, target_sq_here, context_sq_here), "head"
    )
    along, shrink, spread = contrast_terms(products, target_sq, context_sq, loss_weight)
    cand_grads = along[:, :, None] * context[:, None, :] - shrink[:, :, None] * cands
    context_grad = (
        jnp.einsum("mk,mke->me", along, cands, precision=lax.Precision.HIGHEST)
        - spread[:, None] * context
    )
    target_grad = (
        jnp.zeros((frame_count, target_width), jnp.float32).at[local_mask].add(cand_grads[:, 0])
    )
    outgoing = jnp.dot(
        place_b,
        cand_grads[:, 1:].reshape(request_count, target_width).astype(jnp.bfloat16),
        preferred_element_type=jnp.float32,
    ).astype(jnp.bfloat16)
    incoming = lax.all_to_all(
        outgoing.reshape(seq_count, capacity, target_width),
        SEQ,
        split_axis=0,
        concat_axis=0,
        tiled=True,
    ).reshape(slot_total, target_width)
    target_grad = target_grad + jnp.einsum(
        "bf,bw->fw", pick, incoming, preferred_element_type=jnp.float32
    )
    proj_term = jnp.einsum(
        "mw,me->we", masked_full.astype(jnp.float32), context_grad, precision=lax.Precision.HIGHEST
    )
    proj_grad = seq_sum(proj_term, SEQ)
    return (encoded, proj_grad, target_grad)


def solution(mesh):
    seq_size, head_size = mesh.shape["seq"], mesh.shape["head"]
    split_mesh = Mesh(mesh.devices.reshape(seq_size // 2, 2, head_size), ("sz", "sx", "head"))
    return jax.shard_map(
        per_device,
        mesh=split_mesh,
        in_specs=(
            P(SEQ, "head"),
            P("head", None, None),
            P(),
            P(),
            P("head", None),
            P("head", None),
            P("head", None),
            P("head", None),
            P(None, "head"),
            P(SEQ, "head"),
            P(SEQ),
            P(SEQ, None),
            P(SEQ),
        ),
        out_specs=(P(SEQ, "head"), P(None, "head"), P(SEQ, "head")),
        check_vma=False,
    )
```

```python
import math

import jax
import jax.numpy as jnp
from jax import lax
from jax.sharding import Mesh, PartitionSpec as P

TAPS = 128
SEQ = ("sz", "sx")
Y_RING = 4


NORM_EPS = 1e-05
EPSILON = 1e-06
SOFTMAX_WARMTH = 0.1


def with_halo(shard, sides, width):
    for axis, dim in sides:
        size, length = (lax.axis_size(axis), shard.shape[dim])
        up = [(i, (i + 1) % size) for i in range(size - 1)]
        down = [(j, i) for i, j in up]
        last = lax.slice_in_dim(shard, length - width, length, axis=dim)
        first = lax.slice_in_dim(shard, 0, width, axis=dim)
        before = lax.ppermute(last, axis, up)
        after = lax.ppermute(first, axis, down)
        shard = jnp.concatenate([before, shard, after], axis=dim)
    return shard


def layer_norm(hidden, gain_terms, bias_terms):
    wide = hidden.astype(jnp.float32)
    center = jnp.mean(wide, axis=-1, keepdims=True)
    spread = jnp.mean((wide - center) ** 2, axis=-1, keepdims=True)
    return ((wide - center) * lax.rsqrt(spread + NORM_EPS) * gain_terms + bias_terms).astype(
        jnp.bfloat16
    )


def head_project(normed, flat_weight, head_count, head_dim):
    full_width = normed.shape[1]
    head_weight = flat_weight.reshape(head_count, full_width, head_dim)
    result = jnp.einsum("tw,hwd->thd", normed, head_weight, preferred_element_type=jnp.float32)
    return result.astype(jnp.bfloat16)


def contrast_terms(products, target_sq, context_sq, weight_matrix):
    inv_context = lax.rsqrt(context_sq + EPSILON)
    inv_target = lax.rsqrt(target_sq + EPSILON)
    cosine_scores = products * inv_context[:, None] * inv_target
    exponentiated = jnp.exp(cosine_scores / SOFTMAX_WARMTH)
    softmax_shares = exponentiated / jnp.sum(exponentiated, axis=1, keepdims=True)
    leading_term = (lax.broadcasted_iota(jnp.int32, softmax_shares.shape, 1) == 0).astype(
        jnp.float32
    )
    logit_slope = weight_matrix[:, None] * (softmax_shares - leading_term) / SOFTMAX_WARMTH
    along = logit_slope * inv_context[:, None] * inv_target
    shrink = logit_slope * cosine_scores * inv_target * inv_target
    spread = jnp.sum(logit_slope * cosine_scores, axis=1) * inv_context * inv_context
    return (along, shrink, spread)


def attend_block(running, key_block, value_block, query_heads, head_count, score_scale):
    numer, denom, highest = running
    row_count = key_block.shape[0]
    key_heads = key_block.reshape(row_count, head_count, -1)
    value_heads = value_block.reshape(row_count, head_count, -1)
    scores = (
        jnp.einsum("qhd,khd->hqk", query_heads, key_heads, preferred_element_type=jnp.float32)
        * score_scale
    )
    new_high = jnp.maximum(highest, jnp.max(scores, axis=2))
    factor = jnp.exp(highest - new_high)
    weights = jnp.exp(scores - new_high[:, :, None])
    denom = denom * factor + jnp.sum(weights, axis=2)
    numer = numer * factor[:, :, None] + jnp.einsum(
        "hqk,khd->hqd",
        weights.astype(jnp.bfloat16),
        value_heads,
        preferred_element_type=jnp.float32,
    )
    return (numer, denom, new_high)


def take_rows(asked, targets):
    return targets[jnp.maximum(asked, 0)]


def place_rows(asked_flat, rows_flat, frame_count):
    segment_ids = jnp.where(asked_flat >= 0, asked_flat, frame_count)
    return jax.ops.segment_sum(rows_flat, segment_ids, num_segments=frame_count + 1)[:frame_count]


def ring_gather(block, axis, inner):
    size = lax.axis_size(axis)
    outer = size // inner

    def shift(step_outer, step_inner):
        return [
            (i, ((i // inner + step_outer) % outer) * inner + (i % inner + step_inner) % inner)
            for i in range(size)
        ]

    def both_ways(piece, count, up, down):
        parts = [piece]
        left, right = piece, piece
        for _ in range(1, (count + 1) // 2):
            left = lax.ppermute(left, axis, up)
            right = lax.ppermute(right, axis, down)
            parts += [left, right]
        if count % 2 == 0 and count > 1:
            parts.append(lax.ppermute(left, axis, up))
        return jnp.concatenate(parts, axis=0)

    group = both_ways(block, inner, shift(0, 1), shift(0, -1))
    return both_ways(group, outer, shift(1, 0), shift(-1, 0))


def seq_sum(term, axis):
    size = lax.axis_size(axis)
    rows, cols = term.shape
    chunk = -(-rows // size)
    padded = jnp.pad(term, ((0, chunk * size - rows), (0, 0))).reshape(size, chunk, cols)
    reduced = lax.all_to_all(padded, axis, 0, 0, tiled=True).sum(axis=0)
    copies = jnp.broadcast_to(reduced[None], (size, chunk, cols))
    gathered = lax.all_to_all(copies, axis, 0, 0, tiled=True)
    return gathered.reshape(size * chunk, cols)[:rows]


def per_device(
    features,
    conv_weight,
    ln_gain,
    ln_bias,
    query_weight,
    key_weight,
    value_weight,
    out_weight,
    proj_weight,
    targets,
    mask_positions,
    distractors,
    loss_weight,
):
    frame_count, local_width = features.shape
    head_dim = conv_weight.shape[1]
    head_count = local_width // head_dim
    extended = with_halo(features, ((SEQ, 0),), TAPS // 2)
    position = lax.conv_general_dilated(
        extended[None],
        conv_weight,
        (1,),
        "VALID",
        dimension_numbers=("NWC", "OIW", "NWC"),
        feature_group_count=head_count,
        preferred_element_type=jnp.float32,
    )[0, :frame_count]
    hidden = (features.astype(jnp.float32) + jax.nn.gelu(position, approximate=False)).astype(
        jnp.bfloat16
    )
    normed = layer_norm(lax.all_gather(hidden, "head", axis=1, tiled=True), ln_gain, ln_bias)
    query_here = head_project(normed, query_weight, head_count, head_dim).reshape(
        frame_count, local_width
    )
    key_here = head_project(normed, key_weight, head_count, head_dim).reshape(
        frame_count, local_width
    )
    value_here = head_project(normed, value_weight, head_count, head_dim).reshape(
        frame_count, local_width
    )
    side = lax.axis_index("sx")
    swap = [(0, 1), (1, 0)]
    qkv = jnp.stack([query_here, key_here, value_here]).reshape(3, frame_count, head_count, head_dim)
    mine = jnp.where(side == 0, qkv[:, :, 0], qkv[:, :, 1])
    theirs = jnp.where(side == 0, qkv[:, :, 1], qkv[:, :, 0])
    received = lax.ppermute(theirs, "sx", swap)
    pair = jnp.concatenate([mine, received], axis=1)
    kv_pair = jnp.concatenate([pair[1], pair[2]], axis=1)
    if lax.axis_size("sz") % Y_RING == 0:
        kv_all = ring_gather(kv_pair, "sz", Y_RING)
    else:
        kv_all = lax.all_gather(kv_pair, "sz", axis=0, tiled=True)
    key_piece = kv_all[:, :head_dim]
    value_piece = kv_all[:, head_dim:]
    score_scale = 1.0 / math.sqrt(head_dim)
    scores = (
        jnp.einsum("qd,kd->qk", pair[0], key_piece, preferred_element_type=jnp.float32)
        * score_scale
    )
    highest = jnp.max(scores, axis=1, keepdims=True)
    weights = jnp.exp(scores - highest)
    totals = jnp.sum(weights, axis=1, keepdims=True)
    numer = jnp.dot(weights.astype(jnp.bfloat16), value_piece, preferred_element_type=jnp.float32)
    attended_pair = (numer / totals).astype(jnp.bfloat16)
    own_part = attended_pair[:frame_count]
    back = lax.ppermute(attended_pair[frame_count:], "sx", swap)
    attended = jnp.where(
        side == 0,
        jnp.concatenate([own_part, back], axis=1),
        jnp.concatenate([back, own_part], axis=1),
    )
    branch = lax.psum_scatter(
        jnp.dot(attended, out_weight, preferred_element_type=jnp.float32).astype(jnp.bfloat16),
        "head",
        scatter_dimension=1,
        tiled=True,
    ).astype(jnp.float32)
    encoded = (hidden.astype(jnp.float32) + branch).astype(jnp.bfloat16)
    seq_index = lax.axis_index(SEQ)
    seq_count = lax.axis_size(SEQ)
    local_mask = mask_positions - seq_index * frame_count
    masked_full = lax.all_gather(encoded[local_mask], "head", axis=1, tiled=True)
    context = jnp.dot(masked_full, proj_weight, preferred_element_type=jnp.float32)
    masked_count, distract_count = distractors.shape
    request_count = masked_count * distract_count
    capacity = 2 * request_count // seq_count
    target_width = targets.shape[1]
    flat_dist = distractors.reshape(-1)
    owners = flat_dist // frame_count
    row_ids = flat_dist % frame_count
    owner_hits = owners[:, None] == jnp.arange(seq_count, dtype=jnp.int32)[None, :]
    hits = owner_hits.astype(jnp.bfloat16).reshape(masked_count, distract_count, seq_count)
    before = lax.broadcasted_iota(jnp.int32, (distract_count,) * 2, 0) > lax.broadcasted_iota(
        jnp.int32, (distract_count,) * 2, 1
    )
    within = jnp.einsum(
        "kj,mjs->mks", before.astype(jnp.bfloat16), hits, preferred_element_type=jnp.float32
    )
    row_totals = jnp.sum(hits.astype(jnp.float32), axis=1)
    rows_before = lax.broadcasted_iota(jnp.int32, (masked_count,) * 2, 0) > lax.broadcasted_iota(
        jnp.int32, (masked_count,) * 2, 1
    )
    prior = jnp.dot(
        rows_before.astype(jnp.float32), row_totals, precision=lax.Precision.HIGHEST
    )
    earlier = (within + prior[:, None, :]).reshape(request_count, seq_count)
    slot_ids = jnp.sum(jnp.where(owner_hits, earlier, 0.0), axis=1).astype(jnp.int32)
    buckets = owners * capacity + slot_ids
    slot_total = seq_count * capacity
    place = lax.broadcasted_iota(jnp.int32, (slot_total, request_count), 0) == buckets[None, :]
    place_b = place.astype(jnp.bfloat16)
    requests = (
        jnp.sum(jnp.where(place, row_ids[None, :] + 1, 0), axis=1) - 1
    ).reshape(seq_count, capacity)
    positive = targets[local_mask]
    asked = lax.all_to_all(requests, SEQ, split_axis=0, concat_axis=0, tiled=True)
    pick = (
        asked.reshape(-1)[:, None] == jnp.arange(frame_count, dtype=jnp.int32)[None, :]
    ).astype(jnp.bfloat16)
    found = jnp.dot(pick, targets, preferred_element_type=jnp.float32).astype(jnp.bfloat16)
    returned = lax.all_to_all(
        found.reshape(seq_count, capacity, target_width),
        SEQ,
        split_axis=0,
        concat_axis=0,
        tiled=True,
    )
    fetched = jnp.einsum(
        "br,bw->rw",
        place_b,
        returned.reshape(slot_total, target_width),
        preferred_element_type=jnp.float32,
    ).reshape(masked_count, distract_count, target_width)
    cands = jnp.concatenate([positive[:, None, :], fetched], axis=1).astype(jnp.float32)
    products_here = jnp.einsum("me,mke->mk", context, cands, precision=lax.Precision.HIGHEST)
    target_sq_here = jnp.sum(cands * cands, axis=2)
    context_sq_here = jnp.sum(context * context, axis=1)
    products, target_sq, context_sq = lax.psum(
        (products_here, target_sq_here, context_sq_here), "head"
    )
    along, shrink, spread = contrast_terms(products, target_sq, context_sq, loss_weight)
    cand_grads = along[:, :, None] * context[:, None, :] - shrink[:, :, None] * cands
    context_grad = (
        jnp.einsum("mk,mke->me", along, cands, precision=lax.Precision.HIGHEST)
        - spread[:, None] * context
    )
    target_grad = (
        jnp.zeros((frame_count, target_width), jnp.float32).at[local_mask].add(cand_grads[:, 0])
    )
    outgoing = jnp.dot(
        place_b,
        cand_grads[:, 1:].reshape(request_count, target_width).astype(jnp.bfloat16),
        preferred_element_type=jnp.float32,
    ).astype(jnp.bfloat16)
    incoming = lax.all_to_all(
        outgoing.reshape(seq_count, capacity, target_width),
        SEQ,
        split_axis=0,
        concat_axis=0,
        tiled=True,
    ).reshape(slot_total, target_width)
    target_grad = target_grad + jnp.einsum(
        "bf,bw->fw", pick, incoming, preferred_element_type=jnp.float32
    )
    proj_term = jnp.einsum(
        "mw,me->we", masked_full.astype(jnp.float32), context_grad, precision=lax.Precision.HIGHEST
    )
    proj_grad = seq_sum(proj_term, SEQ)
    return (encoded, proj_grad, target_grad)


def solution(mesh):
    seq_size, head_size = mesh.shape["seq"], mesh.shape["head"]
    split_mesh = Mesh(mesh.devices.reshape(seq_size // 2, 2, head_size), ("sz", "sx", "head"))
    return jax.shard_map(
        per_device,
        mesh=split_mesh,
        in_specs=(
            P(SEQ, "head"),
            P("head", None, None),
            P(),
            P(),
            P("head", None),
            P("head", None),
            P("head", None),
            P("head", None),
            P(None, "head"),
            P(SEQ, "head"),
            P(SEQ),
            P(SEQ, None),
            P(SEQ),
        ),
        out_specs=(P(SEQ, "head"), P(None, "head"), P(SEQ, "head")),
        check_vma=False,
    )
```

```python
import math

import jax
import jax.numpy as jnp
from jax import lax
from jax.sharding import Mesh, PartitionSpec as P

TAPS = 128
SEQ = ("sz", "sx")
Y_RING = 4


NORM_EPS = 1e-05
EPSILON = 1e-06
SOFTMAX_WARMTH = 0.1


def with_halo(shard, sides, width):
    for axis, dim in sides:
        size, length = (lax.axis_size(axis), shard.shape[dim])
        up = [(i, (i + 1) % size) for i in range(size - 1)]
        down = [(j, i) for i, j in up]
        last = lax.slice_in_dim(shard, length - width, length, axis=dim)
        first = lax.slice_in_dim(shard, 0, width, axis=dim)
        before = lax.ppermute(last, axis, up)
        after = lax.ppermute(first, axis, down)
        shard = jnp.concatenate([before, shard, after], axis=dim)
    return shard


def layer_norm(hidden, gain_terms, bias_terms):
    wide = hidden.astype(jnp.float32)
    center = jnp.mean(wide, axis=-1, keepdims=True)
    spread = jnp.mean((wide - center) ** 2, axis=-1, keepdims=True)
    return ((wide - center) * lax.rsqrt(spread + NORM_EPS) * gain_terms + bias_terms).astype(
        jnp.bfloat16
    )


def head_project(normed, flat_weight, head_count, head_dim):
    full_width = normed.shape[1]
    head_weight = flat_weight.reshape(head_count, full_width, head_dim)
    result = jnp.einsum("tw,hwd->thd", normed, head_weight, preferred_element_type=jnp.float32)
    return result.astype(jnp.bfloat16)


def contrast_terms(products, target_sq, context_sq, weight_matrix):
    inv_context = lax.rsqrt(context_sq + EPSILON)
    inv_target = lax.rsqrt(target_sq + EPSILON)
    cosine_scores = products * inv_context[:, None] * inv_target
    exponentiated = jnp.exp(cosine_scores / SOFTMAX_WARMTH)
    softmax_shares = exponentiated / jnp.sum(exponentiated, axis=1, keepdims=True)
    leading_term = (lax.broadcasted_iota(jnp.int32, softmax_shares.shape, 1) == 0).astype(
        jnp.float32
    )
    logit_slope = weight_matrix[:, None] * (softmax_shares - leading_term) / SOFTMAX_WARMTH
    along = logit_slope * inv_context[:, None] * inv_target
    shrink = logit_slope * cosine_scores * inv_target * inv_target
    spread = jnp.sum(logit_slope * cosine_scores, axis=1) * inv_context * inv_context
    return (along, shrink, spread)


def attend_block(running, key_block, value_block, query_heads, head_count, score_scale):
    numer, denom, highest = running
    row_count = key_block.shape[0]
    key_heads = key_block.reshape(row_count, head_count, -1)
    value_heads = value_block.reshape(row_count, head_count, -1)
    scores = (
        jnp.einsum("qhd,khd->hqk", query_heads, key_heads, preferred_element_type=jnp.float32)
        * score_scale
    )
    new_high = jnp.maximum(highest, jnp.max(scores, axis=2))
    factor = jnp.exp(highest - new_high)
    weights = jnp.exp(scores - new_high[:, :, None])
    denom = denom * factor + jnp.sum(weights, axis=2)
    numer = numer * factor[:, :, None] + jnp.einsum(
        "hqk,khd->hqd",
        weights.astype(jnp.bfloat16),
        value_heads,
        preferred_element_type=jnp.float32,
    )
    return (numer, denom, new_high)


def take_rows(asked, targets):
    return targets[jnp.maximum(asked, 0)]


def place_rows(asked_flat, rows_flat, frame_count):
    segment_ids = jnp.where(asked_flat >= 0, asked_flat, frame_count)
    return jax.ops.segment_sum(rows_flat, segment_ids, num_segments=frame_count + 1)[:frame_count]


def ring_gather(block, axis, inner):
    size = lax.axis_size(axis)
    outer = size // inner

    def shift(step_outer, step_inner):
        return [
            (i, ((i // inner + step_outer) % outer) * inner + (i % inner + step_inner) % inner)
            for i in range(size)
        ]

    def both_ways(piece, count, up, down):
        parts = [piece]
        left, right = piece, piece
        for _ in range(1, (count + 1) // 2):
            left = lax.ppermute(left, axis, up)
            right = lax.ppermute(right, axis, down)
            parts += [left, right]
        if count % 2 == 0 and count > 1:
            parts.append(lax.ppermute(left, axis, up))
        return jnp.concatenate(parts, axis=0)

    group = both_ways(block, inner, shift(0, 1), shift(0, -1))
    return both_ways(group, outer, shift(1, 0), shift(-1, 0))


def flip_pairs(size, bit):
    return [(i, i ^ bit) for i in range(size)]


def head_scatter_sum(partial, axis):
    size, index = lax.axis_size(axis), lax.axis_index(axis)
    if size & (size - 1):
        return lax.psum_scatter(partial, axis, scatter_dimension=1, tiled=True).astype(jnp.float32)
    current, bit = partial, size // 2
    while bit >= 1:
        half = current.shape[1] // 2
        upper = (index // bit) % 2 == 1
        low, high = current[:, :half], current[:, half:]
        keep = jnp.where(upper, high, low)
        give = jnp.where(upper, low, high)
        got = lax.ppermute(give, axis, flip_pairs(size, bit))
        current = keep.astype(jnp.float32) + got.astype(jnp.float32)
        bit //= 2
    return current.astype(jnp.float32)


def head_sum(values, axis):
    size = lax.axis_size(axis)
    if size & (size - 1):
        return lax.psum(values, axis)
    bit = 1
    while bit < size:
        got = lax.ppermute(values, axis, flip_pairs(size, bit))
        values = jax.tree.map(jnp.add, values, got)
        bit *= 2
    return values


def seq_sum(term, axis):
    size = lax.axis_size(axis)
    rows, cols = term.shape
    chunk = -(-rows // size)
    padded = jnp.pad(term, ((0, chunk * size - rows), (0, 0))).reshape(size, chunk, cols)
    reduced = lax.all_to_all(padded, axis, 0, 0, tiled=True).sum(axis=0)
    copies = jnp.broadcast_to(reduced[None], (size, chunk, cols))
    gathered = lax.all_to_all(copies, axis, 0, 0, tiled=True)
    return gathered.reshape(size * chunk, cols)[:rows]


def per_device(
    features,
    conv_weight,
    ln_gain,
    ln_bias,
    query_weight,
    key_weight,
    value_weight,
    out_weight,
    proj_weight,
    targets,
    mask_positions,
    distractors,
    loss_weight,
):
    frame_count, local_width = features.shape
    head_dim = conv_weight.shape[1]
    head_count = local_width // head_dim
    extended = with_halo(features, ((SEQ, 0),), TAPS // 2)
    position = lax.conv_general_dilated(
        extended[None],
        conv_weight,
        (1,),
        "VALID",
        dimension_numbers=("NWC", "OIW", "NWC"),
        feature_group_count=head_count,
        preferred_element_type=jnp.float32,
    )[0, :frame_count]
    hidden = (features.astype(jnp.float32) + jax.nn.gelu(position, approximate=False)).astype(
        jnp.bfloat16
    )
    normed = layer_norm(lax.all_gather(hidden, "head", axis=1, tiled=True), ln_gain, ln_bias)
    query_here = head_project(normed, query_weight, head_count, head_dim).reshape(
        frame_count, local_width
    )
    key_here = head_project(normed, key_weight, head_count, head_dim).reshape(
        frame_count, local_width
    )
    value_here = head_project(normed, value_weight, head_count, head_dim).reshape(
        frame_count, local_width
    )
    side = lax.axis_index("sx")
    swap = [(0, 1), (1, 0)]
    qkv = jnp.stack([query_here, key_here, value_here]).reshape(3, frame_count, head_count, head_dim)
    mine = jnp.where(side == 0, qkv[:, :, 0], qkv[:, :, 1])
    theirs = jnp.where(side == 0, qkv[:, :, 1], qkv[:, :, 0])
    received = lax.ppermute(theirs, "sx", swap)
    pair = jnp.concatenate([mine, received], axis=1)
    kv_pair = jnp.concatenate([pair[1], pair[2]], axis=1)
    if lax.axis_size("sz") % Y_RING == 0:
        kv_all = ring_gather(kv_pair, "sz", Y_RING)
    else:
        kv_all = lax.all_gather(kv_pair, "sz", axis=0, tiled=True)
    key_piece = kv_all[:, :head_dim]
    value_piece = kv_all[:, head_dim:]
    score_scale = 1.0 / math.sqrt(head_dim)
    scores = (
        jnp.einsum("qd,kd->qk", pair[0], key_piece, preferred_element_type=jnp.float32)
        * score_scale
    )
    highest = jnp.max(scores, axis=1, keepdims=True)
    weights = jnp.exp(scores - highest)
    totals = jnp.sum(weights, axis=1, keepdims=True)
    numer = jnp.dot(weights.astype(jnp.bfloat16), value_piece, preferred_element_type=jnp.float32)
    attended_pair = (numer / totals).astype(jnp.bfloat16)
    own_part = attended_pair[:frame_count]
    back = lax.ppermute(attended_pair[frame_count:], "sx", swap)
    attended = jnp.where(
        side == 0,
        jnp.concatenate([own_part, back], axis=1),
        jnp.concatenate([back, own_part], axis=1),
    )
    branch = head_scatter_sum(
        jnp.dot(attended, out_weight, preferred_element_type=jnp.float32).astype(jnp.bfloat16),
        "head",
    )
    encoded = (hidden.astype(jnp.float32) + branch).astype(jnp.bfloat16)
    seq_index = lax.axis_index(SEQ)
    seq_count = lax.axis_size(SEQ)
    local_mask = mask_positions - seq_index * frame_count
    masked_full = lax.all_gather(encoded[local_mask], "head", axis=1, tiled=True)
    context = jnp.dot(masked_full, proj_weight, preferred_element_type=jnp.float32)
    masked_count, distract_count = distractors.shape
    request_count = masked_count * distract_count
    capacity = 2 * request_count // seq_count
    target_width = targets.shape[1]
    flat_dist = distractors.reshape(-1)
    owners = flat_dist // frame_count
    row_ids = flat_dist % frame_count
    owner_hits = owners[:, None] == jnp.arange(seq_count, dtype=jnp.int32)[None, :]
    hits = owner_hits.astype(jnp.bfloat16).reshape(masked_count, distract_count, seq_count)
    before = lax.broadcasted_iota(jnp.int32, (distract_count,) * 2, 0) > lax.broadcasted_iota(
        jnp.int32, (distract_count,) * 2, 1
    )
    within = jnp.einsum(
        "kj,mjs->mks", before.astype(jnp.bfloat16), hits, preferred_element_type=jnp.float32
    )
    row_totals = jnp.sum(hits.astype(jnp.float32), axis=1)
    rows_before = lax.broadcasted_iota(jnp.int32, (masked_count,) * 2, 0) > lax.broadcasted_iota(
        jnp.int32, (masked_count,) * 2, 1
    )
    prior = jnp.dot(
        rows_before.astype(jnp.float32), row_totals, precision=lax.Precision.HIGHEST
    )
    earlier = (within + prior[:, None, :]).reshape(request_count, seq_count)
    slot_ids = jnp.sum(jnp.where(owner_hits, earlier, 0.0), axis=1).astype(jnp.int32)
    buckets = owners * capacity + slot_ids
    slot_total = seq_count * capacity
    place = lax.broadcasted_iota(jnp.int32, (slot_total, request_count), 0) == buckets[None, :]
    place_b = place.astype(jnp.bfloat16)
    requests = (
        jnp.sum(jnp.where(place, row_ids[None, :] + 1, 0), axis=1) - 1
    ).reshape(seq_count, capacity)
    positive = targets[local_mask]
    asked = lax.all_to_all(requests, SEQ, split_axis=0, concat_axis=0, tiled=True)
    pick = (
        asked.reshape(-1)[:, None] == jnp.arange(frame_count, dtype=jnp.int32)[None, :]
    ).astype(jnp.bfloat16)
    found = jnp.dot(pick, targets, preferred_element_type=jnp.float32).astype(jnp.bfloat16)
    returned = lax.all_to_all(
        found.reshape(seq_count, capacity, target_width),
        SEQ,
        split_axis=0,
        concat_axis=0,
        tiled=True,
    )
    fetched = jnp.einsum(
        "br,bw->rw",
        place_b,
        returned.reshape(slot_total, target_width),
        preferred_element_type=jnp.float32,
    ).reshape(masked_count, distract_count, target_width)
    cands = jnp.concatenate([positive[:, None, :], fetched], axis=1).astype(jnp.float32)
    products_here = jnp.einsum("me,mke->mk", context, cands, precision=lax.Precision.HIGHEST)
    target_sq_here = jnp.sum(cands * cands, axis=2)
    context_sq_here = jnp.sum(context * context, axis=1)
    cand_count = products_here.shape[1]
    summed = head_sum(
        jnp.concatenate([products_here, target_sq_here, context_sq_here[:, None]], axis=1), "head"
    )
    products = summed[:, :cand_count]
    target_sq = summed[:, cand_count : 2 * cand_count]
    context_sq = summed[:, 2 * cand_count]
    along, shrink, spread = contrast_terms(products, target_sq, context_sq, loss_weight)
    cand_grads = along[:, :, None] * context[:, None, :] - shrink[:, :, None] * cands
    context_grad = (
        jnp.einsum("mk,mke->me", along, cands, precision=lax.Precision.HIGHEST)
        - spread[:, None] * context
    )
    target_grad = (
        jnp.zeros((frame_count, target_width), jnp.float32).at[local_mask].add(cand_grads[:, 0])
    )
    outgoing = jnp.dot(
        place_b,
        cand_grads[:, 1:].reshape(request_count, target_width).astype(jnp.bfloat16),
        preferred_element_type=jnp.float32,
    ).astype(jnp.bfloat16)
    incoming = lax.all_to_all(
        outgoing.reshape(seq_count, capacity, target_width),
        SEQ,
        split_axis=0,
        concat_axis=0,
        tiled=True,
    ).reshape(slot_total, target_width)
    target_grad = target_grad + jnp.einsum(
        "bf,bw->fw", pick, incoming, preferred_element_type=jnp.float32
    )
    proj_term = jnp.einsum(
        "mw,me->we", masked_full.astype(jnp.float32), context_grad, precision=lax.Precision.HIGHEST
    )
    proj_grad = seq_sum(proj_term, SEQ)
    return (encoded, proj_grad, target_grad)


def solution(mesh):
    seq_size, head_size = mesh.shape["seq"], mesh.shape["head"]
    split_mesh = Mesh(mesh.devices.reshape(seq_size // 2, 2, head_size), ("sz", "sx", "head"))
    return jax.shard_map(
        per_device,
        mesh=split_mesh,
        in_specs=(
            P(SEQ, "head"),
            P("head", None, None),
            P(),
            P(),
            P("head", None),
            P("head", None),
            P("head", None),
            P("head", None),
            P(None, "head"),
            P(SEQ, "head"),
            P(SEQ),
            P(SEQ, None),
            P(SEQ),
        ),
        out_specs=(P(SEQ, "head"), P(None, "head"), P(SEQ, "head")),
        check_vma=False,
    )
```

```python
import math

import jax
import jax.numpy as jnp
from jax import lax
from jax.sharding import Mesh, PartitionSpec as P

TAPS = 128
SEQ = ("sz", "sx")
Y_RING = 4


NORM_EPS = 1e-05
EPSILON = 1e-06
SOFTMAX_WARMTH = 0.1


def with_halo(shard, sides, width):
    for axis, dim in sides:
        size, length = (lax.axis_size(axis), shard.shape[dim])
        up = [(i, (i + 1) % size) for i in range(size - 1)]
        down = [(j, i) for i, j in up]
        last = lax.slice_in_dim(shard, length - width, length, axis=dim)
        first = lax.slice_in_dim(shard, 0, width, axis=dim)
        before = lax.ppermute(last, axis, up)
        after = lax.ppermute(first, axis, down)
        shard = jnp.concatenate([before, shard, after], axis=dim)
    return shard


def layer_norm(hidden, gain_terms, bias_terms):
    wide = hidden.astype(jnp.float32)
    center = jnp.mean(wide, axis=-1, keepdims=True)
    spread = jnp.mean((wide - center) ** 2, axis=-1, keepdims=True)
    return ((wide - center) * lax.rsqrt(spread + NORM_EPS) * gain_terms + bias_terms).astype(
        jnp.bfloat16
    )


def head_project(normed, flat_weight, head_count, head_dim):
    full_width = normed.shape[1]
    head_weight = flat_weight.reshape(head_count, full_width, head_dim)
    result = jnp.einsum("tw,hwd->thd", normed, head_weight, preferred_element_type=jnp.float32)
    return result.astype(jnp.bfloat16)


def contrast_terms(products, target_sq, context_sq, weight_matrix):
    inv_context = lax.rsqrt(context_sq + EPSILON)
    inv_target = lax.rsqrt(target_sq + EPSILON)
    cosine_scores = products * inv_context[:, None] * inv_target
    exponentiated = jnp.exp(cosine_scores / SOFTMAX_WARMTH)
    softmax_shares = exponentiated / jnp.sum(exponentiated, axis=1, keepdims=True)
    leading_term = (lax.broadcasted_iota(jnp.int32, softmax_shares.shape, 1) == 0).astype(
        jnp.float32
    )
    logit_slope = weight_matrix[:, None] * (softmax_shares - leading_term) / SOFTMAX_WARMTH
    along = logit_slope * inv_context[:, None] * inv_target
    shrink = logit_slope * cosine_scores * inv_target * inv_target
    spread = jnp.sum(logit_slope * cosine_scores, axis=1) * inv_context * inv_context
    return (along, shrink, spread)


def attend_block(running, key_block, value_block, query_heads, head_count, score_scale):
    numer, denom, highest = running
    row_count = key_block.shape[0]
    key_heads = key_block.reshape(row_count, head_count, -1)
    value_heads = value_block.reshape(row_count, head_count, -1)
    scores = (
        jnp.einsum("qhd,khd->hqk", query_heads, key_heads, preferred_element_type=jnp.float32)
        * score_scale
    )
    new_high = jnp.maximum(highest, jnp.max(scores, axis=2))
    factor = jnp.exp(highest - new_high)
    weights = jnp.exp(scores - new_high[:, :, None])
    denom = denom * factor + jnp.sum(weights, axis=2)
    numer = numer * factor[:, :, None] + jnp.einsum(
        "hqk,khd->hqd",
        weights.astype(jnp.bfloat16),
        value_heads,
        preferred_element_type=jnp.float32,
    )
    return (numer, denom, new_high)


def take_rows(asked, targets):
    return targets[jnp.maximum(asked, 0)]


def place_rows(asked_flat, rows_flat, frame_count):
    segment_ids = jnp.where(asked_flat >= 0, asked_flat, frame_count)
    return jax.ops.segment_sum(rows_flat, segment_ids, num_segments=frame_count + 1)[:frame_count]


def ring_gather(block, axis, inner):
    size = lax.axis_size(axis)
    outer = size // inner

    def shift(step_outer, step_inner):
        return [
            (i, ((i // inner + step_outer) % outer) * inner + (i % inner + step_inner) % inner)
            for i in range(size)
        ]

    def both_ways(piece, count, up, down):
        parts = [piece]
        left, right = piece, piece
        for _ in range(1, (count + 1) // 2):
            left = lax.ppermute(left, axis, up)
            right = lax.ppermute(right, axis, down)
            parts += [left, right]
        if count % 2 == 0 and count > 1:
            parts.append(lax.ppermute(left, axis, up))
        return jnp.concatenate(parts, axis=0)

    group = both_ways(block, inner, shift(0, 1), shift(0, -1))
    return both_ways(group, outer, shift(1, 0), shift(-1, 0))


def flip_pairs(size, bit):
    return [(i, i ^ bit) for i in range(size)]


def head_scatter_sum(partial, axis):
    size, index = lax.axis_size(axis), lax.axis_index(axis)
    if size & (size - 1):
        return lax.psum_scatter(partial, axis, scatter_dimension=1, tiled=True).astype(jnp.float32)
    current, bit = partial, size // 2
    while bit >= 1:
        half = current.shape[1] // 2
        upper = (index // bit) % 2 == 1
        low, high = current[:, :half], current[:, half:]
        keep = jnp.where(upper, high, low)
        give = jnp.where(upper, low, high)
        got = lax.ppermute(give, axis, flip_pairs(size, bit))
        current = keep.astype(jnp.float32) + got.astype(jnp.float32)
        bit //= 2
    return current.astype(jnp.float32)


def head_sum(values, axis):
    size = lax.axis_size(axis)
    if size & (size - 1):
        return lax.psum(values, axis)
    bit = 1
    while bit < size:
        got = lax.ppermute(values, axis, flip_pairs(size, bit))
        values = jax.tree.map(jnp.add, values, got)
        bit *= 2
    return values


def seq_sum(term, axis):
    size = lax.axis_size(axis)
    rows, cols = term.shape
    chunk = -(-rows // size)
    padded = jnp.pad(term, ((0, chunk * size - rows), (0, 0))).reshape(size, chunk, cols)
    reduced = lax.all_to_all(padded, axis, 0, 0, tiled=True).sum(axis=0)
    copies = jnp.broadcast_to(reduced[None], (size, chunk, cols))
    gathered = lax.all_to_all(copies, axis, 0, 0, tiled=True)
    return gathered.reshape(size * chunk, cols)[:rows]


def per_device(
    features,
    conv_weight,
    ln_gain,
    ln_bias,
    query_weight,
    key_weight,
    value_weight,
    out_weight,
    proj_weight,
    targets,
    mask_positions,
    distractors,
    loss_weight,
):
    frame_count, local_width = features.shape
    head_dim = conv_weight.shape[1]
    head_count = local_width // head_dim
    extended = with_halo(features, ((SEQ, 0),), TAPS // 2)
    position = lax.conv_general_dilated(
        extended[None],
        conv_weight,
        (1,),
        "VALID",
        dimension_numbers=("NWC", "OIW", "NWC"),
        feature_group_count=head_count,
        preferred_element_type=jnp.float32,
    )[0, :frame_count]
    hidden = (features.astype(jnp.float32) + jax.nn.gelu(position, approximate=False)).astype(
        jnp.bfloat16
    )
    normed = layer_norm(lax.all_gather(hidden, "head", axis=1, tiled=True), ln_gain, ln_bias)
    query_here = head_project(normed, query_weight, head_count, head_dim).reshape(
        frame_count, local_width
    )
    key_here = head_project(normed, key_weight, head_count, head_dim).reshape(
        frame_count, local_width
    )
    value_here = head_project(normed, value_weight, head_count, head_dim).reshape(
        frame_count, local_width
    )
    side = lax.axis_index("sx")
    swap = [(0, 1), (1, 0)]
    qkv = jnp.stack([query_here, key_here, value_here]).reshape(3, frame_count, head_count, head_dim)
    mine = jnp.where(side == 0, qkv[:, :, 0], qkv[:, :, 1])
    theirs = jnp.where(side == 0, qkv[:, :, 1], qkv[:, :, 0])
    received = lax.ppermute(theirs, "sx", swap)
    pair = jnp.concatenate([mine, received], axis=1)
    kv_pair = jnp.concatenate([pair[1], pair[2]], axis=1)
    if lax.axis_size("sz") % Y_RING == 0:
        kv_all = ring_gather(kv_pair, "sz", Y_RING)
    else:
        kv_all = lax.all_gather(kv_pair, "sz", axis=0, tiled=True)
    key_piece = kv_all[:, :head_dim]
    value_piece = kv_all[:, head_dim:]
    score_scale = 1.0 / math.sqrt(head_dim)
    scores = (
        jnp.einsum("qd,kd->qk", pair[0], key_piece, preferred_element_type=jnp.float32)
        * score_scale
    )
    highest = jnp.max(scores, axis=1, keepdims=True)
    weights = jnp.exp(scores - highest)
    totals = jnp.sum(weights, axis=1, keepdims=True)
    numer = jnp.dot(weights.astype(jnp.bfloat16), value_piece, preferred_element_type=jnp.float32)
    attended_pair = (numer / totals).astype(jnp.bfloat16)
    own_part = attended_pair[:frame_count]
    back = lax.ppermute(attended_pair[frame_count:], "sx", swap)
    attended = jnp.where(
        side == 0,
        jnp.concatenate([own_part, back], axis=1),
        jnp.concatenate([back, own_part], axis=1),
    )
    branch = head_scatter_sum(
        jnp.dot(attended, out_weight, preferred_element_type=jnp.float32).astype(jnp.bfloat16),
        "head",
    )
    encoded = (hidden.astype(jnp.float32) + branch).astype(jnp.bfloat16)
    seq_index = lax.axis_index(SEQ)
    seq_count = lax.axis_size(SEQ)
    local_mask = mask_positions - seq_index * frame_count
    masked_full = lax.all_gather(encoded[local_mask], "head", axis=1, tiled=True)
    context = jnp.dot(masked_full, proj_weight, preferred_element_type=jnp.float32)
    masked_count, distract_count = distractors.shape
    request_count = masked_count * distract_count
    capacity = 2 * request_count // seq_count
    target_width = targets.shape[1]
    flat_dist = distractors.reshape(-1)
    owners = flat_dist // frame_count
    row_ids = flat_dist % frame_count
    owner_hits = owners[:, None] == jnp.arange(seq_count, dtype=jnp.int32)[None, :]
    hits = owner_hits.astype(jnp.bfloat16).reshape(masked_count, distract_count, seq_count)
    before = lax.broadcasted_iota(jnp.int32, (distract_count,) * 2, 0) > lax.broadcasted_iota(
        jnp.int32, (distract_count,) * 2, 1
    )
    within = jnp.einsum(
        "kj,mjs->mks", before.astype(jnp.bfloat16), hits, preferred_element_type=jnp.float32
    )
    row_totals = jnp.sum(hits.astype(jnp.float32), axis=1)
    rows_before = lax.broadcasted_iota(jnp.int32, (masked_count,) * 2, 0) > lax.broadcasted_iota(
        jnp.int32, (masked_count,) * 2, 1
    )
    prior = jnp.dot(
        rows_before.astype(jnp.float32), row_totals, precision=lax.Precision.HIGHEST
    )
    earlier = (within + prior[:, None, :]).reshape(request_count, seq_count)
    slot_ids = jnp.sum(jnp.where(owner_hits, earlier, 0.0), axis=1).astype(jnp.int32)
    buckets = owners * capacity + slot_ids
    slot_total = seq_count * capacity
    place = lax.broadcasted_iota(jnp.int32, (slot_total, request_count), 0) == buckets[None, :]
    place_b = place.astype(jnp.bfloat16)
    requests = (
        jnp.sum(jnp.where(place, row_ids[None, :] + 1, 0), axis=1) - 1
    ).reshape(seq_count, capacity)
    positive = targets[local_mask]
    asked = lax.all_to_all(requests, SEQ, split_axis=0, concat_axis=0, tiled=True)
    pick = (
        asked.reshape(-1)[:, None] == jnp.arange(frame_count, dtype=jnp.int32)[None, :]
    ).astype(jnp.bfloat16)
    found = jnp.dot(pick, targets, preferred_element_type=jnp.float32).astype(jnp.bfloat16)
    returned = lax.all_to_all(
        found.reshape(seq_count, capacity, target_width),
        SEQ,
        split_axis=0,
        concat_axis=0,
        tiled=True,
    )
    fetched = jnp.einsum(
        "br,bw->rw",
        place_b,
        returned.reshape(slot_total, target_width),
        preferred_element_type=jnp.float32,
    ).reshape(masked_count, distract_count, target_width)
    cands = jnp.concatenate([positive[:, None, :], fetched], axis=1).astype(jnp.float32)
    products_here = jnp.einsum("me,mke->mk", context, cands, precision=lax.Precision.HIGHEST)
    target_sq_here = jnp.sum(cands * cands, axis=2)
    context_sq_here = jnp.sum(context * context, axis=1)
    cand_count = products_here.shape[1]
    summed = head_sum(
        jnp.concatenate([products_here, target_sq_here, context_sq_here[:, None]], axis=1), "head"
    )
    products = summed[:, :cand_count]
    target_sq = summed[:, cand_count : 2 * cand_count]
    context_sq = summed[:, 2 * cand_count]
    along, shrink, spread = contrast_terms(products, target_sq, context_sq, loss_weight)
    cand_grads = along[:, :, None] * context[:, None, :] - shrink[:, :, None] * cands
    context_grad = (
        jnp.einsum("mk,mke->me", along, cands, precision=lax.Precision.HIGHEST)
        - spread[:, None] * context
    )
    target_grad = (
        jnp.zeros((frame_count, target_width), jnp.float32).at[local_mask].add(cand_grads[:, 0])
    )
    outgoing = jnp.dot(
        place_b,
        cand_grads[:, 1:].reshape(request_count, target_width).astype(jnp.bfloat16),
        preferred_element_type=jnp.float32,
    ).astype(jnp.bfloat16)
    proj_term = jnp.einsum(
        "mw,me->we", masked_full.astype(jnp.float32), context_grad, precision=lax.Precision.HIGHEST
    )
    proj_rows, proj_cols = proj_term.shape
    chunk = -(-proj_rows // seq_count)
    proj_parts = (
        jnp.pad(proj_term, ((0, chunk * seq_count - proj_rows), (0, 0)))
        .astype(jnp.bfloat16)
        .reshape(seq_count, chunk, proj_cols)
    )
    outgoing = outgoing.reshape(seq_count, capacity, target_width)
    if proj_cols == target_width:
        got = lax.all_to_all(
            jnp.concatenate([outgoing, proj_parts], axis=1), SEQ, 0, 0, tiled=True
        )
        incoming, proj_got = got[:, :capacity], got[:, capacity:]
    else:
        incoming = lax.all_to_all(outgoing, SEQ, 0, 0, tiled=True)
        proj_got = lax.all_to_all(proj_parts, SEQ, 0, 0, tiled=True)
    incoming = incoming.reshape(slot_total, target_width)
    target_grad = target_grad + jnp.einsum(
        "bf,bw->fw", pick, incoming, preferred_element_type=jnp.float32
    )
    reduced = jnp.sum(proj_got.astype(jnp.float32), axis=0).astype(jnp.bfloat16)
    copies = jnp.broadcast_to(reduced[None], (seq_count, chunk, proj_cols))
    proj_grad = (
        lax.all_to_all(copies, SEQ, 0, 0, tiled=True)
        .reshape(seq_count * chunk, proj_cols)[:proj_rows]
        .astype(jnp.float32)
    )
    return (encoded, proj_grad, target_grad)


def solution(mesh):
    seq_size, head_size = mesh.shape["seq"], mesh.shape["head"]
    split_mesh = Mesh(mesh.devices.reshape(seq_size // 2, 2, head_size), ("sz", "sx", "head"))
    return jax.shard_map(
        per_device,
        mesh=split_mesh,
        in_specs=(
            P(SEQ, "head"),
            P("head", None, None),
            P(),
            P(),
            P("head", None),
            P("head", None),
            P("head", None),
            P("head", None),
            P(None, "head"),
            P(SEQ, "head"),
            P(SEQ),
            P(SEQ, None),
            P(SEQ),
        ),
        out_specs=(P(SEQ, "head"), P(None, "head"), P(SEQ, "head")),
        check_vma=False,
    )
```

```python
import math

import jax
import jax.numpy as jnp
from jax import lax
from jax.sharding import Mesh, PartitionSpec as P

TAPS = 128
SEQ = ("sz", "sx")
Y_RING = 4


NORM_EPS = 1e-05
EPSILON = 1e-06
SOFTMAX_WARMTH = 0.1


def with_halo(shard, sides, width):
    for axis, dim in sides:
        size, length = (lax.axis_size(axis), shard.shape[dim])
        up = [(i, (i + 1) % size) for i in range(size - 1)]
        down = [(j, i) for i, j in up]
        last = lax.slice_in_dim(shard, length - width, length, axis=dim)
        first = lax.slice_in_dim(shard, 0, width, axis=dim)
        before = lax.ppermute(last, axis, up)
        after = lax.ppermute(first, axis, down)
        shard = jnp.concatenate([before, shard, after], axis=dim)
    return shard


def layer_norm(hidden, gain_terms, bias_terms):
    wide = hidden.astype(jnp.float32)
    center = jnp.mean(wide, axis=-1, keepdims=True)
    spread = jnp.mean((wide - center) ** 2, axis=-1, keepdims=True)
    return ((wide - center) * lax.rsqrt(spread + NORM_EPS) * gain_terms + bias_terms).astype(
        jnp.bfloat16
    )


def head_project(normed, flat_weight, head_count, head_dim):
    full_width = normed.shape[1]
    head_weight = flat_weight.reshape(head_count, full_width, head_dim)
    result = jnp.einsum("tw,hwd->thd", normed, head_weight, preferred_element_type=jnp.float32)
    return result.astype(jnp.bfloat16)


def contrast_terms(products, target_sq, context_sq, weight_matrix):
    inv_context = lax.rsqrt(context_sq + EPSILON)
    inv_target = lax.rsqrt(target_sq + EPSILON)
    cosine_scores = products * inv_context[:, None] * inv_target
    exponentiated = jnp.exp(cosine_scores / SOFTMAX_WARMTH)
    softmax_shares = exponentiated / jnp.sum(exponentiated, axis=1, keepdims=True)
    leading_term = (lax.broadcasted_iota(jnp.int32, softmax_shares.shape, 1) == 0).astype(
        jnp.float32
    )
    logit_slope = weight_matrix[:, None] * (softmax_shares - leading_term) / SOFTMAX_WARMTH
    along = logit_slope * inv_context[:, None] * inv_target
    shrink = logit_slope * cosine_scores * inv_target * inv_target
    spread = jnp.sum(logit_slope * cosine_scores, axis=1) * inv_context * inv_context
    return (along, shrink, spread)


def attend_block(running, key_block, value_block, query_heads, head_count, score_scale):
    numer, denom, highest = running
    row_count = key_block.shape[0]
    key_heads = key_block.reshape(row_count, head_count, -1)
    value_heads = value_block.reshape(row_count, head_count, -1)
    scores = (
        jnp.einsum("qhd,khd->hqk", query_heads, key_heads, preferred_element_type=jnp.float32)
        * score_scale
    )
    new_high = jnp.maximum(highest, jnp.max(scores, axis=2))
    factor = jnp.exp(highest - new_high)
    weights = jnp.exp(scores - new_high[:, :, None])
    denom = denom * factor + jnp.sum(weights, axis=2)
    numer = numer * factor[:, :, None] + jnp.einsum(
        "hqk,khd->hqd",
        weights.astype(jnp.bfloat16),
        value_heads,
        preferred_element_type=jnp.float32,
    )
    return (numer, denom, new_high)


def take_rows(asked, targets):
    return targets[jnp.maximum(asked, 0)]


def place_rows(asked_flat, rows_flat, frame_count):
    segment_ids = jnp.where(asked_flat >= 0, asked_flat, frame_count)
    return jax.ops.segment_sum(rows_flat, segment_ids, num_segments=frame_count + 1)[:frame_count]


def ring_gather(block, axis, inner):
    size = lax.axis_size(axis)
    outer = size // inner

    def shift(step_outer, step_inner):
        return [
            (i, ((i // inner + step_outer) % outer) * inner + (i % inner + step_inner) % inner)
            for i in range(size)
        ]

    def both_ways(piece, count, up, down):
        parts = [piece]
        left, right = piece, piece
        for _ in range(1, (count + 1) // 2):
            left = lax.ppermute(left, axis, up)
            right = lax.ppermute(right, axis, down)
            parts += [left, right]
        if count % 2 == 0 and count > 1:
            parts.append(lax.ppermute(left, axis, up))
        return jnp.concatenate(parts, axis=0)

    group = both_ways(block, inner, shift(0, 1), shift(0, -1))
    return both_ways(group, outer, shift(1, 0), shift(-1, 0))


def flip_pairs(size, bit):
    return [(i, i ^ bit) for i in range(size)]


def head_scatter_sum(partial, axis):
    size, index = lax.axis_size(axis), lax.axis_index(axis)
    if size & (size - 1):
        return lax.psum_scatter(partial, axis, scatter_dimension=1, tiled=True).astype(jnp.float32)
    current, bit = partial, size // 2
    while bit >= 1:
        half = current.shape[1] // 2
        upper = (index // bit) % 2 == 1
        low, high = current[:, :half], current[:, half:]
        keep = jnp.where(upper, high, low)
        give = jnp.where(upper, low, high)
        got = lax.ppermute(give, axis, flip_pairs(size, bit))
        current = keep.astype(jnp.float32) + got.astype(jnp.float32)
        bit //= 2
    return current.astype(jnp.float32)


def head_sum(values, axis):
    size = lax.axis_size(axis)
    if size & (size - 1):
        return lax.psum(values, axis)
    bit = 1
    while bit < size:
        got = lax.ppermute(values, axis, flip_pairs(size, bit))
        values = jax.tree.map(jnp.add, values, got)
        bit *= 2
    return values


def seq_sum(term, axis):
    size = lax.axis_size(axis)
    rows, cols = term.shape
    chunk = -(-rows // size)
    padded = jnp.pad(term, ((0, chunk * size - rows), (0, 0))).reshape(size, chunk, cols)
    reduced = lax.all_to_all(padded, axis, 0, 0, tiled=True).sum(axis=0)
    copies = jnp.broadcast_to(reduced[None], (size, chunk, cols))
    gathered = lax.all_to_all(copies, axis, 0, 0, tiled=True)
    return gathered.reshape(size * chunk, cols)[:rows]


def per_device(
    features,
    conv_weight,
    ln_gain,
    ln_bias,
    query_weight,
    key_weight,
    value_weight,
    out_weight,
    proj_weight,
    targets,
    mask_positions,
    distractors,
    loss_weight,
):
    frame_count, local_width = features.shape
    head_dim = conv_weight.shape[1]
    head_count = local_width // head_dim
    extended = with_halo(features, ((SEQ, 0),), TAPS // 2)
    ext_rows = extended.shape[0]
    taps = conv_weight.shape[2]
    window_shape = (ext_rows, frame_count, taps)
    shift = (
        lax.broadcasted_iota(jnp.int32, window_shape, 0)
        == lax.broadcasted_iota(jnp.int32, window_shape, 1)
        + lax.broadcasted_iota(jnp.int32, window_shape, 2)
    ).astype(jnp.bfloat16)
    windows = jnp.einsum(
        "sgi,stu->gtiu",
        extended.reshape(ext_rows, head_count, head_dim),
        shift,
        preferred_element_type=jnp.float32,
    ).astype(jnp.bfloat16)
    position = jnp.einsum(
        "gtiu,goiu->tgo",
        windows,
        conv_weight.reshape(head_count, head_dim, head_dim, taps),
        preferred_element_type=jnp.float32,
    ).reshape(frame_count, local_width)
    hidden = (features.astype(jnp.float32) + jax.nn.gelu(position, approximate=False)).astype(
        jnp.bfloat16
    )
    normed = layer_norm(lax.all_gather(hidden, "head", axis=1, tiled=True), ln_gain, ln_bias)
    query_here = head_project(normed, query_weight, head_count, head_dim).reshape(
        frame_count, local_width
    )
    key_here = head_project(normed, key_weight, head_count, head_dim).reshape(
        frame_count, local_width
    )
    value_here = head_project(normed, value_weight, head_count, head_dim).reshape(
        frame_count, local_width
    )
    side = lax.axis_index("sx")
    swap = [(0, 1), (1, 0)]
    qkv = jnp.stack([query_here, key_here, value_here]).reshape(3, frame_count, head_count, head_dim)
    mine = jnp.where(side == 0, qkv[:, :, 0], qkv[:, :, 1])
    theirs = jnp.where(side == 0, qkv[:, :, 1], qkv[:, :, 0])
    received = lax.ppermute(theirs, "sx", swap)
    pair = jnp.concatenate([mine, received], axis=1)
    kv_pair = jnp.concatenate([pair[1], pair[2]], axis=1)
    if lax.axis_size("sz") % Y_RING == 0:
        kv_all = ring_gather(kv_pair, "sz", Y_RING)
    else:
        kv_all = lax.all_gather(kv_pair, "sz", axis=0, tiled=True)
    key_piece = kv_all[:, :head_dim]
    value_piece = kv_all[:, head_dim:]
    score_scale = 1.0 / math.sqrt(head_dim)
    scores = (
        jnp.einsum("qd,kd->qk", pair[0], key_piece, preferred_element_type=jnp.float32)
        * score_scale
    )
    highest = jnp.max(scores, axis=1, keepdims=True)
    weights = jnp.exp(scores - highest)
    totals = jnp.sum(weights, axis=1, keepdims=True)
    numer = jnp.dot(weights.astype(jnp.bfloat16), value_piece, preferred_element_type=jnp.float32)
    attended_pair = (numer / totals).astype(jnp.bfloat16)
    own_part = attended_pair[:frame_count]
    back = lax.ppermute(attended_pair[frame_count:], "sx", swap)
    attended = jnp.where(
        side == 0,
        jnp.concatenate([own_part, back], axis=1),
        jnp.concatenate([back, own_part], axis=1),
    )
    branch = head_scatter_sum(
        jnp.dot(attended, out_weight, preferred_element_type=jnp.float32).astype(jnp.bfloat16),
        "head",
    )
    encoded = (hidden.astype(jnp.float32) + branch).astype(jnp.bfloat16)
    seq_index = lax.axis_index(SEQ)
    seq_count = lax.axis_size(SEQ)
    local_mask = mask_positions - seq_index * frame_count
    masked_full = lax.all_gather(encoded[local_mask], "head", axis=1, tiled=True)
    context = jnp.dot(masked_full, proj_weight, preferred_element_type=jnp.float32)
    masked_count, distract_count = distractors.shape
    request_count = masked_count * distract_count
    capacity = 2 * request_count // seq_count
    target_width = targets.shape[1]
    flat_dist = distractors.reshape(-1)
    owners = flat_dist // frame_count
    row_ids = flat_dist % frame_count
    owner_hits = owners[:, None] == jnp.arange(seq_count, dtype=jnp.int32)[None, :]
    hits = owner_hits.astype(jnp.bfloat16).reshape(masked_count, distract_count, seq_count)
    before = lax.broadcasted_iota(jnp.int32, (distract_count,) * 2, 0) > lax.broadcasted_iota(
        jnp.int32, (distract_count,) * 2, 1
    )
    within = jnp.einsum(
        "kj,mjs->mks", before.astype(jnp.bfloat16), hits, preferred_element_type=jnp.float32
    )
    row_totals = jnp.sum(hits.astype(jnp.float32), axis=1)
    rows_before = lax.broadcasted_iota(jnp.int32, (masked_count,) * 2, 0) > lax.broadcasted_iota(
        jnp.int32, (masked_count,) * 2, 1
    )
    prior = jnp.dot(
        rows_before.astype(jnp.float32), row_totals, precision=lax.Precision.HIGHEST
    )
    earlier = (within + prior[:, None, :]).reshape(request_count, seq_count)
    slot_ids = jnp.sum(jnp.where(owner_hits, earlier, 0.0), axis=1).astype(jnp.int32)
    buckets = owners * capacity + slot_ids
    slot_total = seq_count * capacity
    place = lax.broadcasted_iota(jnp.int32, (slot_total, request_count), 0) == buckets[None, :]
    place_b = place.astype(jnp.bfloat16)
    requests = (
        jnp.sum(jnp.where(place, row_ids[None, :] + 1, 0), axis=1) - 1
    ).reshape(seq_count, capacity)
    positive = targets[local_mask]
    asked = lax.all_to_all(requests, SEQ, split_axis=0, concat_axis=0, tiled=True)
    pick = (
        asked.reshape(-1)[:, None] == jnp.arange(frame_count, dtype=jnp.int32)[None, :]
    ).astype(jnp.bfloat16)
    found = jnp.dot(pick, targets, preferred_element_type=jnp.float32).astype(jnp.bfloat16)
    returned = lax.all_to_all(
        found.reshape(seq_count, capacity, target_width),
        SEQ,
        split_axis=0,
        concat_axis=0,
        tiled=True,
    )
    fetched = jnp.einsum(
        "br,bw->rw",
        place_b,
        returned.reshape(slot_total, target_width),
        preferred_element_type=jnp.float32,
    ).reshape(masked_count, distract_count, target_width)
    cands = jnp.concatenate([positive[:, None, :], fetched], axis=1).astype(jnp.float32)
    products_here = jnp.einsum("me,mke->mk", context, cands, precision=lax.Precision.HIGHEST)
    target_sq_here = jnp.sum(cands * cands, axis=2)
    context_sq_here = jnp.sum(context * context, axis=1)
    cand_count = products_here.shape[1]
    summed = head_sum(
        jnp.concatenate([products_here, target_sq_here, context_sq_here[:, None]], axis=1), "head"
    )
    products = summed[:, :cand_count]
    target_sq = summed[:, cand_count : 2 * cand_count]
    context_sq = summed[:, 2 * cand_count]
    along, shrink, spread = contrast_terms(products, target_sq, context_sq, loss_weight)
    cand_grads = along[:, :, None] * context[:, None, :] - shrink[:, :, None] * cands
    context_grad = (
        jnp.einsum("mk,mke->me", along, cands, precision=lax.Precision.HIGHEST)
        - spread[:, None] * context
    )
    target_grad = (
        jnp.zeros((frame_count, target_width), jnp.float32).at[local_mask].add(cand_grads[:, 0])
    )
    outgoing = jnp.dot(
        place_b,
        cand_grads[:, 1:].reshape(request_count, target_width).astype(jnp.bfloat16),
        preferred_element_type=jnp.float32,
    ).astype(jnp.bfloat16)
    proj_term = jnp.einsum(
        "mw,me->we", masked_full.astype(jnp.float32), context_grad, precision=lax.Precision.HIGHEST
    )
    proj_rows, proj_cols = proj_term.shape
    chunk = -(-proj_rows // seq_count)
    proj_parts = (
        jnp.pad(proj_term, ((0, chunk * seq_count - proj_rows), (0, 0)))
        .astype(jnp.bfloat16)
        .reshape(seq_count, chunk, proj_cols)
    )
    outgoing = outgoing.reshape(seq_count, capacity, target_width)
    if proj_cols == target_width:
        got = lax.all_to_all(
            jnp.concatenate([outgoing, proj_parts], axis=1), SEQ, 0, 0, tiled=True
        )
        incoming, proj_got = got[:, :capacity], got[:, capacity:]
    else:
        incoming = lax.all_to_all(outgoing, SEQ, 0, 0, tiled=True)
        proj_got = lax.all_to_all(proj_parts, SEQ, 0, 0, tiled=True)
    incoming = incoming.reshape(slot_total, target_width)
    target_grad = target_grad + jnp.einsum(
        "bf,bw->fw", pick, incoming, preferred_element_type=jnp.float32
    )
    reduced = jnp.sum(proj_got.astype(jnp.float32), axis=0).astype(jnp.bfloat16)
    copies = jnp.broadcast_to(reduced[None], (seq_count, chunk, proj_cols))
    proj_grad = (
        lax.all_to_all(copies, SEQ, 0, 0, tiled=True)
        .reshape(seq_count * chunk, proj_cols)[:proj_rows]
        .astype(jnp.float32)
    )
    return (encoded, proj_grad, target_grad)


def solution(mesh):
    seq_size, head_size = mesh.shape["seq"], mesh.shape["head"]
    split_mesh = Mesh(mesh.devices.reshape(seq_size // 2, 2, head_size), ("sz", "sx", "head"))
    return jax.shard_map(
        per_device,
        mesh=split_mesh,
        in_specs=(
            P(SEQ, "head"),
            P("head", None, None),
            P(),
            P(),
            P("head", None),
            P("head", None),
            P("head", None),
            P("head", None),
            P(None, "head"),
            P(SEQ, "head"),
            P(SEQ),
            P(SEQ, None),
            P(SEQ),
        ),
        out_specs=(P(SEQ, "head"), P(None, "head"), P(SEQ, "head")),
        check_vma=False,
    )
```

```python
import math

import jax
import jax.numpy as jnp
from jax import lax
from jax.sharding import Mesh, PartitionSpec as P

TAPS = 128
SEQ = ("sz", "sx")
Y_RING = 4


NORM_EPS = 1e-05
EPSILON = 1e-06
SOFTMAX_WARMTH = 0.1


def with_halo(shard, sides, width):
    for axis, dim in sides:
        size, length = (lax.axis_size(axis), shard.shape[dim])
        up = [(i, (i + 1) % size) for i in range(size - 1)]
        down = [(j, i) for i, j in up]
        last = lax.slice_in_dim(shard, length - width, length, axis=dim)
        first = lax.slice_in_dim(shard, 0, width, axis=dim)
        before = lax.ppermute(last, axis, up)
        after = lax.ppermute(first, axis, down)
        shard = jnp.concatenate([before, shard, after], axis=dim)
    return shard


def layer_norm(hidden, gain_terms, bias_terms):
    wide = hidden.astype(jnp.float32)
    center = jnp.mean(wide, axis=-1, keepdims=True)
    spread = jnp.mean((wide - center) ** 2, axis=-1, keepdims=True)
    return ((wide - center) * lax.rsqrt(spread + NORM_EPS) * gain_terms + bias_terms).astype(
        jnp.bfloat16
    )


def head_project(normed, flat_weight, head_count, head_dim):
    full_width = normed.shape[1]
    head_weight = flat_weight.reshape(head_count, full_width, head_dim)
    result = jnp.einsum("tw,hwd->thd", normed, head_weight, preferred_element_type=jnp.float32)
    return result.astype(jnp.bfloat16)


def contrast_terms(products, target_sq, context_sq, weight_matrix):
    inv_context = lax.rsqrt(context_sq + EPSILON)
    inv_target = lax.rsqrt(target_sq + EPSILON)
    cosine_scores = products * inv_context[:, None] * inv_target
    exponentiated = jnp.exp(cosine_scores / SOFTMAX_WARMTH)
    softmax_shares = exponentiated / jnp.sum(exponentiated, axis=1, keepdims=True)
    leading_term = (lax.broadcasted_iota(jnp.int32, softmax_shares.shape, 1) == 0).astype(
        jnp.float32
    )
    logit_slope = weight_matrix[:, None] * (softmax_shares - leading_term) / SOFTMAX_WARMTH
    along = logit_slope * inv_context[:, None] * inv_target
    shrink = logit_slope * cosine_scores * inv_target * inv_target
    spread = jnp.sum(logit_slope * cosine_scores, axis=1) * inv_context * inv_context
    return (along, shrink, spread)


def attend_block(running, key_block, value_block, query_heads, head_count, score_scale):
    numer, denom, highest = running
    row_count = key_block.shape[0]
    key_heads = key_block.reshape(row_count, head_count, -1)
    value_heads = value_block.reshape(row_count, head_count, -1)
    scores = (
        jnp.einsum("qhd,khd->hqk", query_heads, key_heads, preferred_element_type=jnp.float32)
        * score_scale
    )
    new_high = jnp.maximum(highest, jnp.max(scores, axis=2))
    factor = jnp.exp(highest - new_high)
    weights = jnp.exp(scores - new_high[:, :, None])
    denom = denom * factor + jnp.sum(weights, axis=2)
    numer = numer * factor[:, :, None] + jnp.einsum(
        "hqk,khd->hqd",
        weights.astype(jnp.bfloat16),
        value_heads,
        preferred_element_type=jnp.float32,
    )
    return (numer, denom, new_high)


def take_rows(asked, targets):
    return targets[jnp.maximum(asked, 0)]


def place_rows(asked_flat, rows_flat, frame_count):
    segment_ids = jnp.where(asked_flat >= 0, asked_flat, frame_count)
    return jax.ops.segment_sum(rows_flat, segment_ids, num_segments=frame_count + 1)[:frame_count]


def ring_gather(block, axis, inner):
    size = lax.axis_size(axis)
    outer = size // inner

    def shift(step_outer, step_inner):
        return [
            (i, ((i // inner + step_outer) % outer) * inner + (i % inner + step_inner) % inner)
            for i in range(size)
        ]

    def both_ways(piece, count, up, down):
        parts = [piece]
        left, right = piece, piece
        for _ in range(1, (count + 1) // 2):
            left = lax.ppermute(left, axis, up)
            right = lax.ppermute(right, axis, down)
            parts += [left, right]
        if count % 2 == 0 and count > 1:
            parts.append(lax.ppermute(left, axis, up))
        return jnp.concatenate(parts, axis=0)

    group = both_ways(block, inner, shift(0, 1), shift(0, -1))
    return both_ways(group, outer, shift(1, 0), shift(-1, 0))


def flip_pairs(size, bit):
    return [(i, i ^ bit) for i in range(size)]


def head_scatter_sum(partial, axis):
    size, index = lax.axis_size(axis), lax.axis_index(axis)
    if size & (size - 1):
        return lax.psum_scatter(partial, axis, scatter_dimension=1, tiled=True).astype(jnp.float32)
    current, bit = partial, size // 2
    while bit >= 1:
        half = current.shape[1] // 2
        upper = (index // bit) % 2 == 1
        low, high = current[:, :half], current[:, half:]
        keep = jnp.where(upper, high, low)
        give = jnp.where(upper, low, high)
        got = lax.ppermute(give, axis, flip_pairs(size, bit))
        current = keep.astype(jnp.float32) + got.astype(jnp.float32)
        bit //= 2
    return current.astype(jnp.float32)


def head_gather(block, axis):
    size, index = lax.axis_size(axis), lax.axis_index(axis)
    if size & (size - 1):
        return lax.all_gather(block, axis, axis=1, tiled=True)
    current, bit = block, 1
    while bit < size:
        got = lax.ppermute(current, axis, flip_pairs(size, bit))
        upper = (index // bit) % 2 == 1
        current = jnp.where(
            upper, jnp.concatenate([got, current], axis=1), jnp.concatenate([current, got], axis=1)
        )
        bit *= 2
    return current


def head_sum(values, axis):
    size = lax.axis_size(axis)
    if size & (size - 1):
        return lax.psum(values, axis)
    bit = 1
    while bit < size:
        got = lax.ppermute(values, axis, flip_pairs(size, bit))
        values = jax.tree.map(jnp.add, values, got)
        bit *= 2
    return values


def seq_sum(term, axis):
    size = lax.axis_size(axis)
    rows, cols = term.shape
    chunk = -(-rows // size)
    padded = jnp.pad(term, ((0, chunk * size - rows), (0, 0))).reshape(size, chunk, cols)
    reduced = lax.all_to_all(padded, axis, 0, 0, tiled=True).sum(axis=0)
    copies = jnp.broadcast_to(reduced[None], (size, chunk, cols))
    gathered = lax.all_to_all(copies, axis, 0, 0, tiled=True)
    return gathered.reshape(size * chunk, cols)[:rows]


def per_device(
    features,
    conv_weight,
    ln_gain,
    ln_bias,
    query_weight,
    key_weight,
    value_weight,
    out_weight,
    proj_weight,
    targets,
    mask_positions,
    distractors,
    loss_weight,
):
    frame_count, local_width = features.shape
    head_dim = conv_weight.shape[1]
    head_count = local_width // head_dim
    extended = with_halo(features, ((SEQ, 0),), TAPS // 2)
    ext_rows = extended.shape[0]
    taps = conv_weight.shape[2]
    window_shape = (ext_rows, frame_count, taps)
    shift = (
        lax.broadcasted_iota(jnp.int32, window_shape, 0)
        == lax.broadcasted_iota(jnp.int32, window_shape, 1)
        + lax.broadcasted_iota(jnp.int32, window_shape, 2)
    ).astype(jnp.bfloat16)
    windows = jnp.einsum(
        "sgi,stu->gtiu",
        extended.reshape(ext_rows, head_count, head_dim),
        shift,
        preferred_element_type=jnp.float32,
    ).astype(jnp.bfloat16)
    position = jnp.einsum(
        "gtiu,goiu->tgo",
        windows,
        conv_weight.reshape(head_count, head_dim, head_dim, taps),
        preferred_element_type=jnp.float32,
    ).reshape(frame_count, local_width)
    hidden = (features.astype(jnp.float32) + jax.nn.gelu(position, approximate=False)).astype(
        jnp.bfloat16
    )
    normed = layer_norm(head_gather(hidden, "head"), ln_gain, ln_bias)
    query_here = head_project(normed, query_weight, head_count, head_dim).reshape(
        frame_count, local_width
    )
    key_here = head_project(normed, key_weight, head_count, head_dim).reshape(
        frame_count, local_width
    )
    value_here = head_project(normed, value_weight, head_count, head_dim).reshape(
        frame_count, local_width
    )
    side = lax.axis_index("sx")
    swap = [(0, 1), (1, 0)]
    qkv = jnp.stack([query_here, key_here, value_here]).reshape(3, frame_count, head_count, head_dim)
    mine = jnp.where(side == 0, qkv[:, :, 0], qkv[:, :, 1])
    theirs = jnp.where(side == 0, qkv[:, :, 1], qkv[:, :, 0])
    received = lax.ppermute(theirs, "sx", swap)
    pair = jnp.concatenate([mine, received], axis=1)
    kv_pair = jnp.concatenate([pair[1], pair[2]], axis=1)
    if lax.axis_size("sz") % Y_RING == 0:
        kv_all = ring_gather(kv_pair, "sz", Y_RING)
    else:
        kv_all = lax.all_gather(kv_pair, "sz", axis=0, tiled=True)
    key_piece = kv_all[:, :head_dim]
    value_piece = kv_all[:, head_dim:]
    score_scale = 1.0 / math.sqrt(head_dim)
    scores = (
        jnp.einsum("qd,kd->qk", pair[0], key_piece, preferred_element_type=jnp.float32)
        * score_scale
    )
    highest = jnp.max(scores, axis=1, keepdims=True)
    weights = jnp.exp(scores - highest)
    totals = jnp.sum(weights, axis=1, keepdims=True)
    numer = jnp.dot(weights.astype(jnp.bfloat16), value_piece, preferred_element_type=jnp.float32)
    attended_pair = (numer / totals).astype(jnp.bfloat16)
    own_part = attended_pair[:frame_count]
    back = lax.ppermute(attended_pair[frame_count:], "sx", swap)
    attended = jnp.where(
        side == 0,
        jnp.concatenate([own_part, back], axis=1),
        jnp.concatenate([back, own_part], axis=1),
    )
    branch = head_scatter_sum(
        jnp.dot(attended, out_weight, preferred_element_type=jnp.float32).astype(jnp.bfloat16),
        "head",
    )
    encoded = (hidden.astype(jnp.float32) + branch).astype(jnp.bfloat16)
    seq_index = lax.axis_index(SEQ)
    seq_count = lax.axis_size(SEQ)
    local_mask = mask_positions - seq_index * frame_count
    masked_full = lax.all_gather(encoded[local_mask], "head", axis=1, tiled=True)
    context = jnp.dot(masked_full, proj_weight, preferred_element_type=jnp.float32)
    masked_count, distract_count = distractors.shape
    request_count = masked_count * distract_count
    capacity = 2 * request_count // seq_count
    target_width = targets.shape[1]
    flat_dist = distractors.reshape(-1)
    owners = flat_dist // frame_count
    row_ids = flat_dist % frame_count
    owner_hits = owners[:, None] == jnp.arange(seq_count, dtype=jnp.int32)[None, :]
    hits = owner_hits.astype(jnp.bfloat16).reshape(masked_count, distract_count, seq_count)
    before = lax.broadcasted_iota(jnp.int32, (distract_count,) * 2, 0) > lax.broadcasted_iota(
        jnp.int32, (distract_count,) * 2, 1
    )
    within = jnp.einsum(
        "kj,mjs->mks", before.astype(jnp.bfloat16), hits, preferred_element_type=jnp.float32
    )
    row_totals = jnp.sum(hits.astype(jnp.float32), axis=1)
    rows_before = lax.broadcasted_iota(jnp.int32, (masked_count,) * 2, 0) > lax.broadcasted_iota(
        jnp.int32, (masked_count,) * 2, 1
    )
    prior = jnp.dot(
        rows_before.astype(jnp.float32), row_totals, precision=lax.Precision.HIGHEST
    )
    earlier = (within + prior[:, None, :]).reshape(request_count, seq_count)
    slot_ids = jnp.sum(jnp.where(owner_hits, earlier, 0.0), axis=1).astype(jnp.int32)
    buckets = owners * capacity + slot_ids
    slot_total = seq_count * capacity
    place = lax.broadcasted_iota(jnp.int32, (slot_total, request_count), 0) == buckets[None, :]
    place_b = place.astype(jnp.bfloat16)
    requests = (
        jnp.sum(jnp.where(place, row_ids[None, :] + 1, 0), axis=1) - 1
    ).reshape(seq_count, capacity)
    positive = targets[local_mask]
    asked = lax.all_to_all(requests, SEQ, split_axis=0, concat_axis=0, tiled=True)
    pick = (
        asked.reshape(-1)[:, None] == jnp.arange(frame_count, dtype=jnp.int32)[None, :]
    ).astype(jnp.bfloat16)
    found = jnp.dot(pick, targets, preferred_element_type=jnp.float32).astype(jnp.bfloat16)
    returned = lax.all_to_all(
        found.reshape(seq_count, capacity, target_width),
        SEQ,
        split_axis=0,
        concat_axis=0,
        tiled=True,
    )
    fetched = jnp.einsum(
        "br,bw->rw",
        place_b,
        returned.reshape(slot_total, target_width),
        preferred_element_type=jnp.float32,
    ).reshape(masked_count, distract_count, target_width)
    cands = jnp.concatenate([positive[:, None, :], fetched], axis=1).astype(jnp.float32)
    products_here = jnp.einsum("me,mke->mk", context, cands, precision=lax.Precision.HIGHEST)
    target_sq_here = jnp.sum(cands * cands, axis=2)
    context_sq_here = jnp.sum(context * context, axis=1)
    cand_count = products_here.shape[1]
    summed = head_sum(
        jnp.concatenate([products_here, target_sq_here, context_sq_here[:, None]], axis=1), "head"
    )
    products = summed[:, :cand_count]
    target_sq = summed[:, cand_count : 2 * cand_count]
    context_sq = summed[:, 2 * cand_count]
    along, shrink, spread = contrast_terms(products, target_sq, context_sq, loss_weight)
    cand_grads = along[:, :, None] * context[:, None, :] - shrink[:, :, None] * cands
    context_grad = (
        jnp.einsum("mk,mke->me", along, cands, precision=lax.Precision.HIGHEST)
        - spread[:, None] * context
    )
    target_grad = (
        jnp.zeros((frame_count, target_width), jnp.float32).at[local_mask].add(cand_grads[:, 0])
    )
    outgoing = jnp.dot(
        place_b,
        cand_grads[:, 1:].reshape(request_count, target_width).astype(jnp.bfloat16),
        preferred_element_type=jnp.float32,
    ).astype(jnp.bfloat16)
    proj_term = jnp.einsum(
        "mw,me->we", masked_full.astype(jnp.float32), context_grad, precision=lax.Precision.HIGHEST
    )
    proj_rows, proj_cols = proj_term.shape
    chunk = -(-proj_rows // seq_count)
    proj_parts = (
        jnp.pad(proj_term, ((0, chunk * seq_count - proj_rows), (0, 0)))
        .astype(jnp.bfloat16)
        .reshape(seq_count, chunk, proj_cols)
    )
    outgoing = outgoing.reshape(seq_count, capacity, target_width)
    if proj_cols == target_width:
        got = lax.all_to_all(
            jnp.concatenate([outgoing, proj_parts], axis=1), SEQ, 0, 0, tiled=True
        )
        incoming, proj_got = got[:, :capacity], got[:, capacity:]
    else:
        incoming = lax.all_to_all(outgoing, SEQ, 0, 0, tiled=True)
        proj_got = lax.all_to_all(proj_parts, SEQ, 0, 0, tiled=True)
    incoming = incoming.reshape(slot_total, target_width)
    target_grad = target_grad + jnp.einsum(
        "bf,bw->fw", pick, incoming, preferred_element_type=jnp.float32
    )
    reduced = jnp.sum(proj_got.astype(jnp.float32), axis=0).astype(jnp.bfloat16)
    copies = jnp.broadcast_to(reduced[None], (seq_count, chunk, proj_cols))
    proj_grad = (
        lax.all_to_all(copies, SEQ, 0, 0, tiled=True)
        .reshape(seq_count * chunk, proj_cols)[:proj_rows]
        .astype(jnp.float32)
    )
    return (encoded, proj_grad, target_grad)


def solution(mesh):
    seq_size, head_size = mesh.shape["seq"], mesh.shape["head"]
    split_mesh = Mesh(mesh.devices.reshape(seq_size // 2, 2, head_size), ("sz", "sx", "head"))
    return jax.shard_map(
        per_device,
        mesh=split_mesh,
        in_specs=(
            P(SEQ, "head"),
            P("head", None, None),
            P(),
            P(),
            P("head", None),
            P("head", None),
            P("head", None),
            P("head", None),
            P(None, "head"),
            P(SEQ, "head"),
            P(SEQ),
            P(SEQ, None),
            P(SEQ),
        ),
        out_specs=(P(SEQ, "head"), P(None, "head"), P(SEQ, "head")),
        check_vma=False,
    )
```
